256 devices in a mesh: pipe: 8 (over z), seq: 8 (over y, core), mp: 4 (over x).
Axes of the slice: x: 4, y: 4, z: 8, core: 2. Of those that a mesh axis runs over, the one named last changes fastest.
Arguments:
- shared_fwd: bfloat16 [8, 2048, 3072], P('pipe', ('seq', 'mp')), may hold values from -7.5 to 7.5
- values_fwd: bfloat16 [8, 2048, 3072], P('pipe', ('seq', 'mp')), may hold values from -6 to 6
- shared_bwd: bfloat16 [8, 2048, 3072], P('pipe', ('seq', 'mp')), may hold values from -7.5 to 7.5
- values_bwd: bfloat16 [8, 2048, 3072], P('pipe', ('seq', 'mp')), may hold values from -6 to 6
- upstream_bwd: bfloat16 [8, 2048, 3072], P('pipe', ('seq', 'mp')), may hold values from -6 to 6
- cluster_order: int32 [8, 2, 2048], P('pipe'), may hold values from 0 to 2047, as said below
Outputs:
- forward_in: bfloat16 [8, 2048, 3072], P('pipe', ('seq', 'mp'))
- shared_grad_in: bfloat16 [8, 2048, 3072], P('pipe', ('seq', 'mp'))
- values_grad_in: bfloat16 [8, 2048, 3072], P('pipe', ('seq', 'mp'))
The draws below stay inside these ranges and needn't reach their ends.
Inputs may be any that keep to these rules, and one draw needn't show every extreme that they name: cluster_order[l, b] is a permutation of the token positions for every layer l and micro-batch b. Cut the slots into blocks of 256 and the positions into ranges of 64: each range fills 0, 8 or 16 slots of each block, and some range fills 16 in some block.
All inputs are finite; a program needn't handle non-finite values.
Results may differ from the reference program's by a relative error of at most 0.007.
Values may be sent and summed in bfloat16 or wider, within the bound.
No kernel may reach another device: no remote copies, remote signals or barrier semaphores. Data moves between devices by JAX's collectives and lax.ppermute only.
A program may use at most 64 MiB of HBM per device.

```python
import math
import jax
import jax.numpy as jnp
from jax import lax

HEADS = 24
HEAD_DIM = 128
CLUSTER = 256
LAYERS = 8
ROWS = 256
TOK_DEV = 64
TOKENS = 2048
N_SEQ = 8
N_MP = 4


def cluster_table(key):
    range_count = N_SEQ * N_MP
    share_rows = ROWS // range_count

    def single_table(subkey):
        pick_key, step_key, range_key, slot_key = jax.random.split(subkey, 4)
        pair_count = N_SEQ // 2
        first_range = jax.random.randint(pick_key, (pair_count,), 0, range_count)
        second_range = (first_range + jax.random.randint(step_key, (pair_count,), 1, range_count)) % range_count
        block_ids = jnp.arange(N_SEQ)
        direction = jnp.where(block_ids % 2 == 0, 1, -1)
        range_ids = jnp.arange(range_count)[:, None]
        gain_here = (range_ids == first_range[block_ids // 2][None, :]).astype(jnp.int32)
        loss_here = (range_ids == second_range[block_ids // 2][None, :]).astype(jnp.int32)
        counts = share_rows + share_rows * direction[None, :] * (gain_here - loss_here)
        offsets = jnp.cumsum(counts, axis=1) - counts
        upper_edge = jnp.cumsum(counts, axis=0)
        lower_edge = upper_edge - counts
        slot_ids = jnp.arange(ROWS)
        source = jnp.sum((slot_ids[None, None, :] >= upper_edge[:, :, None]).astype(jnp.int32), axis=0)
        block_column = block_ids[:, None]
        within = slot_ids[None, :] - lower_edge[source, block_column]
        range_perms = jax.vmap(lambda inner_key: jax.random.permutation(inner_key, TOK_DEV))(jax.random.split(range_key, range_count))
        token_ids = source * TOK_DEV + range_perms[source, offsets[source, block_column] + within]
        slot_perms = jax.vmap(lambda inner_key: jax.random.permutation(inner_key, ROWS))(jax.random.split(slot_key, N_SEQ))
        token_ids = jnp.take_along_axis(token_ids, slot_perms, axis=1)
        return token_ids.reshape(TOKENS).astype(jnp.int32)
    return jax.vmap(single_table)(jax.random.split(key, LAYERS * 2)).reshape(LAYERS, 2, TOKENS)


def drawn_shared(key, micro_index):
    features = HEADS * HEAD_DIM
    value_key = jax.random.fold_in(key, 31 + micro_index)
    base_key = jax.random.fold_in(value_key, 0)
    drawn = jax.random.normal(base_key, (LAYERS, TOKENS, features), jnp.float32)
    return jnp.clip(drawn, -7.5, 7.5).astype(jnp.bfloat16)


def draw_shared_fwd(key, part):
    return drawn_shared(key, 0)


def draw_shared_bwd(key, part):
    return drawn_shared(key, 1)


def draw_cluster_order(key, part):
    return cluster_table(jax.random.fold_in(key, 7))


def level_of(key, dims, shards, least, high):
    level = 1.0
    for axis_at, parts in shards:
        steps = jax.random.uniform(jax.random.fold_in(jax.random.fold_in(key, 6), axis_at), (parts,), jnp.float32, least / len(shards), high / len(shards))
        level = level * jnp.repeat(jnp.exp(steps), dims[axis_at] // parts).reshape((-1,) + (1,) * (len(dims) - 1 - axis_at))
    return level


def scatter_about(key, extent, deviation, reach, cuts=(), kind=jnp.bfloat16):
    values = jax.random.normal(key, extent, jnp.float32) * deviation
    if len(cuts) > 0:
        values = level_of(key, extent, cuts, -0.22, 0.18) * values
    return jnp.clip(values, min=-reach, max=reach).astype(kind)


def setup_inputs(seed: int = 0) -> dict:
    keys = jax.random.split(jax.random.key(seed), 7)
    shared_fwd = draw_shared_fwd(jax.random.fold_in(keys[6], 71), 0)
    values_fwd = scatter_about(keys[1], (LAYERS, TOKENS, HEADS * HEAD_DIM), 1.0, 6.0, ((0, 8), (1, 32)))
    shared_bwd = draw_shared_bwd(jax.random.fold_in(keys[6], 71), 0)
    values_bwd = scatter_about(keys[3], (LAYERS, TOKENS, HEADS * HEAD_DIM), 1.0, 6.0, ((0, 8), (1, 32)))
    upstream_bwd = scatter_about(keys[4], (LAYERS, TOKENS, HEADS * HEAD_DIM), 1.0, 6.0, ((0, 8), (1, 32)))
    cluster_order = draw_cluster_order(jax.random.fold_in(keys[6], 71), 0)
    return dict(shared_fwd=shared_fwd, values_fwd=values_fwd, shared_bwd=shared_bwd, values_bwd=values_bwd, upstream_bwd=upstream_bwd, cluster_order=cluster_order)


MASKED = -1e+30
HIGHEST = lax.Precision.HIGHEST

def visible_mask(positions):
    count = positions.shape[0]
    earlier = positions[None, :] < positions[:, None]
    earliest = positions == jnp.min(positions)
    diagonal = jnp.arange(count)[:, None] == jnp.arange(count)[None, :]
    return earlier | diagonal & earliest[:, None]

def softmax_weights(shared, positions):
    scores = jnp.einsum('qhd,khd->hqk', shared, shared, precision=HIGHEST) * (1.0 / math.sqrt(HEAD_DIM))
    scores = jnp.where(visible_mask(positions)[None], scores, MASKED)
    largest = lax.optimization_barrier(jnp.max(scores, axis=-1, keepdims=True))
    exponent = jnp.exp(scores - largest)
    return exponent / lax.optimization_barrier(jnp.sum(exponent, axis=-1, keepdims=True))

def rounded_copy(array):
    return lax.optimization_barrier(array.astype(jnp.bfloat16)).astype(jnp.float32)

def forward_cluster(block_items):
    shared, values, positions = block_items
    shared = shared.astype(jnp.float32)
    values = values.astype(jnp.float32)
    weights = rounded_copy(softmax_weights(shared, positions))
    attended = jnp.einsum('hqk,khd->qhd', weights, values, precision=HIGHEST)
    return attended.astype(jnp.bfloat16)

def backward_cluster(block_items):
    shared, values, upstream, positions = block_items
    shared = shared.astype(jnp.float32)
    values = values.astype(jnp.float32)
    upstream = upstream.astype(jnp.float32)
    weights = softmax_weights(shared, positions)
    rounded = rounded_copy(weights)
    output_b = jnp.einsum('hqk,khd->qhd', rounded, values, precision=HIGHEST)
    row_delta = lax.optimization_barrier(jnp.sum(upstream * output_b, axis=-1))
    value_grad = jnp.einsum('hqk,qhd->khd', rounded, upstream, precision=HIGHEST)
    prob_grad = jnp.einsum('qhd,khd->hqk', upstream, values, precision=HIGHEST)
    score_grad = weights * (prob_grad - jnp.transpose(row_delta)[:, :, None]) * (1.0 / math.sqrt(HEAD_DIM))
    score_low = rounded_copy(score_grad)
    shared_grad = jnp.einsum('hqk,khd->qhd', score_low, shared, precision=HIGHEST) + jnp.einsum('hqk,qhd->khd', score_low, shared, precision=HIGHEST)
    return (shared_grad.astype(jnp.bfloat16), value_grad.astype(jnp.bfloat16))

def reference(shared_fwd, values_fwd, shared_bwd, values_bwd, upstream_bwd, cluster_order):
    clusters = TOKENS // CLUSTER
    features = HEADS * HEAD_DIM
    forward_list = []
    shared_list = []
    values_list = []
    for segment in range(LAYERS):
        order_fwd = cluster_order[segment, 0].astype(jnp.int32)
        order_bwd = cluster_order[segment, 1].astype(jnp.int32)
        attended = lax.map(forward_cluster, (shared_fwd[segment][order_fwd].reshape(clusters, CLUSTER, HEADS, HEAD_DIM), values_fwd[segment][order_fwd].reshape(clusters, CLUSTER, HEADS, HEAD_DIM), order_fwd.reshape(clusters, CLUSTER)))
        forward_list.append(jnp.zeros((TOKENS, features), jnp.bfloat16).at[order_fwd].set(attended.reshape(TOKENS, features)))
        shared_grad, value_grad = lax.map(backward_cluster, (shared_bwd[segment][order_bwd].reshape(clusters, CLUSTER, HEADS, HEAD_DIM), values_bwd[segment][order_bwd].reshape(clusters, CLUSTER, HEADS, HEAD_DIM), upstream_bwd[segment][order_bwd].reshape(clusters, CLUSTER, HEADS, HEAD_DIM), order_bwd.reshape(clusters, CLUSTER)))
        shared_list.append(jnp.zeros((TOKENS, features), jnp.bfloat16).at[order_bwd].set(shared_grad.reshape(TOKENS, features)))
        values_list.append(jnp.zeros((TOKENS, features), jnp.bfloat16).at[order_bwd].set(value_grad.reshape(TOKENS, features)))
    empty = jnp.zeros((1, TOKENS, features), jnp.bfloat16)
    forward_in = jnp.concatenate([empty, jnp.stack(forward_list[:-1])], axis=0)
    shared_grad_in = jnp.concatenate([jnp.stack(shared_list[1:]), empty], axis=0)
    values_grad_in = jnp.concatenate([jnp.stack(values_list[1:]), empty], axis=0)
    return (forward_in, shared_grad_in, values_grad_in)
```

```python
import math

import jax
import jax.numpy as jnp
from jax import lax
from jax.sharding import PartitionSpec as P

HEAD_DIM = 128
CLUSTER = 256


MASKED = -1e30


def shifted(block, axis, distance):
    devices = range(lax.axis_size(axis))
    route = [(i - distance, i) for i in devices if i - distance in devices]
    return lax.ppermute(block, axis, route)


def visible_mask(positions):
    count = positions.shape[1]
    earlier = positions[:, None, :] < positions[:, :, None]
    earliest = positions == jnp.min(positions, axis=1, keepdims=True)
    diagonal = (jnp.arange(count)[:, None] == jnp.arange(count)[None, :])[None]
    return earlier | diagonal & earliest[:, :, None]


def softmax_weights(shared, positions, score_scale):
    scores = (
        jnp.einsum("nqhd,nkhd->nhqk", shared, shared, preferred_element_type=jnp.float32)
        * score_scale
    )
    scores = jnp.where(visible_mask(positions)[:, None], scores, MASKED)
    largest = jnp.max(scores, axis=-1, keepdims=True)
    exponent = jnp.exp(scores - largest)
    return exponent / jnp.sum(exponent, axis=-1, keepdims=True)


def forward_block(shared, values, positions, score_scale):
    weights = softmax_weights(shared, positions, score_scale).astype(jnp.bfloat16)
    return jnp.einsum(
        "nhqk,nkhd->nqhd", weights, values, preferred_element_type=jnp.float32
    ).astype(jnp.bfloat16)


def backward_block(shared, values, upstream, positions, score_scale):
    weights = softmax_weights(shared, positions, score_scale)
    rounded = weights.astype(jnp.bfloat16)
    output_b = jnp.einsum("nhqk,nkhd->nqhd", rounded, values, preferred_element_type=jnp.float32)
    row_delta = jnp.sum(upstream.astype(jnp.float32) * output_b, axis=-1)
    value_grad = jnp.einsum(
        "nhqk,nqhd->nkhd", rounded, upstream, preferred_element_type=jnp.float32
    ).astype(jnp.bfloat16)
    prob_grad = jnp.einsum("nqhd,nkhd->nhqk", upstream, values, preferred_element_type=jnp.float32)
    score_grad = (
        weights * (prob_grad - jnp.transpose(row_delta, (0, 2, 1))[..., None]) * score_scale
    ).astype(jnp.bfloat16)
    shared_grad = jnp.einsum(
        "nhqk,nkhd->nqhd", score_grad, shared, preferred_element_type=jnp.float32
    )
    shared_grad = shared_grad + jnp.einsum(
        "nhqk,nqhd->nkhd", score_grad, shared, preferred_element_type=jnp.float32
    )
    return (shared_grad.astype(jnp.bfloat16), value_grad)


def route_plan(slot_tokens, seq_index, range_here, seq_count, group_count, tok_dev, slot_count):
    block_rows = slot_tokens.shape[0] // seq_count
    source = slot_tokens // tok_dev
    local_row = (slot_tokens - range_here * tok_dev).reshape(seq_count, block_rows)
    owned_here = (source == range_here).reshape(seq_count, block_rows)
    slot_rank = jnp.cumsum(owned_here.astype(jnp.int32), axis=1) - 1
    selected = owned_here[:, None, :] & (
        slot_rank[:, None, :] == jnp.arange(slot_count)[None, :, None]
    )
    send_rows = jnp.sum(jnp.where(selected, local_row[:, None, :], 0), axis=2)
    filled = jnp.any(selected, axis=2)
    send = filled[:, :, None] & (send_rows[:, :, None] == jnp.arange(tok_dev)[None, None, :])
    block_order = lax.dynamic_slice_in_dim(slot_tokens, seq_index * block_rows, block_rows)
    block_source = block_order // tok_dev
    indicator = (block_source[:, None] == jnp.arange(group_count)[None, :]).astype(jnp.int32)
    block_rank = jnp.sum(jnp.cumsum(indicator, axis=0) * indicator, axis=1) - 1
    gather = (block_source[:, None, None] == jnp.arange(group_count)[None, :, None]) & (
        block_rank[:, None, None] == jnp.arange(slot_count)[None, None, :]
    )
    return (
        send.astype(jnp.bfloat16),
        gather.astype(jnp.bfloat16),
        block_order,
    )


def per_device(shared_fwd, values_fwd, shared_bwd, values_bwd, upstream_bwd, cluster_order):
    seq_count = lax.axis_size("seq")
    mp_count = lax.axis_size("mp")
    seq_index = lax.axis_index("seq")
    mp_index = lax.axis_index("mp")
    tok_dev = shared_fwd.shape[1]
    features = shared_fwd.shape[2]
    group_features = features // mp_count
    heads_dev = group_features // HEAD_DIM
    group_count = seq_count * mp_count
    range_here = seq_index * mp_count + mp_index
    block_rows = cluster_order.shape[2] // seq_count
    slot_count = 2 * block_rows // group_count
    score_scale = 1.0 / math.sqrt(HEAD_DIM)
    axes = ("seq", "mp")
    plan_fwd = route_plan(
        cluster_order[0, 0], seq_index, range_here, seq_count, group_count, tok_dev, slot_count
    )
    plan_bwd = route_plan(
        cluster_order[0, 1], seq_index, range_here, seq_count, group_count, tok_dev, slot_count
    )

    def exchange(arrays, send):
        packed = [
            jnp.einsum(
                "skt,tmf->smkf",
                send,
                array[0].reshape(tok_dev, mp_count, group_features),
                preferred_element_type=jnp.bfloat16,
            )
            for array in arrays
        ]
        stacked = jnp.stack(packed, axis=2).reshape(
            group_count, len(arrays), slot_count, group_features
        )
        return lax.all_to_all(stacked, axes, split_axis=0, concat_axis=0, tiled=True)

    def gather_block(arrived, gather):
        rows = jnp.einsum("irk,rakf->aif", gather, arrived, preferred_element_type=jnp.bfloat16)
        return [row.reshape(1, block_rows, heads_dev, HEAD_DIM) for row in rows]

    def give_back(results, gather, send):
        flat = jnp.stack([r.reshape(block_rows, group_features) for r in results], axis=0)
        placed = jnp.einsum("irk,aif->rakf", gather, flat, preferred_element_type=jnp.bfloat16)
        arrived = lax.all_to_all(placed, axes, split_axis=0, concat_axis=0, tiled=True)
        arrived = arrived.reshape(seq_count, mp_count, len(results), slot_count, group_features)
        rows = jnp.einsum("skt,smakf->atmf", send, arrived, preferred_element_type=jnp.bfloat16)
        return [row.reshape(1, tok_dev, features) for row in rows]

    arrived_f = exchange((shared_fwd, values_fwd), plan_fwd[0])
    arrived_b = exchange((shared_bwd, values_bwd, upstream_bwd), plan_bwd[0])
    positions_f = plan_fwd[2].reshape(-1, CLUSTER)
    positions_b = plan_bwd[2].reshape(-1, CLUSTER)
    shared_f, values_f = gather_block(arrived_f, plan_fwd[1])
    attended = forward_block(shared_f, values_f, positions_f, score_scale)
    (forward_out,) = give_back((attended,), plan_fwd[1], plan_fwd[0])
    forward_in = shifted(forward_out, "pipe", 1)
    shared_b, values_b, upstream_b = gather_block(arrived_b, plan_bwd[1])
    shared_grad, value_grad = backward_block(shared_b, values_b, upstream_b, positions_b, score_scale)
    shared_out, values_out = give_back((shared_grad, value_grad), plan_bwd[1], plan_bwd[0])
    shared_grad_in, values_grad_in = shifted((shared_out, values_out), "pipe", -1)
    return (forward_in, shared_grad_in, values_grad_in)


def solution(mesh):
    in_specs = (
        P("pipe", ("seq", "mp"), None),
        P("pipe", ("seq", "mp"), None),
        P("pipe", ("seq", "mp"), None),
        P("pipe", ("seq", "mp"), None),
        P("pipe", ("seq", "mp"), None),
        P("pipe", None, None),
    )
    out_specs = (
        P("pipe", ("seq", "mp"), None),
        P("pipe", ("seq", "mp"), None),
        P("pipe", ("seq", "mp"), None),
    )
    return jax.shard_map(
        per_device, mesh=mesh, in_specs=in_specs, out_specs=out_specs, check_vma=False
    )
```

```python
import math

import jax
import jax.numpy as jnp
from jax import lax
from jax.sharding import PartitionSpec as P

HEAD_DIM = 128
CLUSTER = 256


MASKED = -1e30


def shifted(block, axis, distance):
    devices = range(lax.axis_size(axis))
    route = [(i - distance, i) for i in devices if i - distance in devices]
    return lax.ppermute(block, axis, route)


def visible_mask(positions):
    count = positions.shape[1]
    earlier = positions[:, None, :] < positions[:, :, None]
    earliest = positions == jnp.min(positions, axis=1, keepdims=True)
    diagonal = (jnp.arange(count)[:, None] == jnp.arange(count)[None, :])[None]
    return earlier | diagonal & earliest[:, :, None]


def softmax_weights(shared, positions, score_scale):
    scores = (
        jnp.einsum("nqhd,nkhd->nhqk", shared, shared, preferred_element_type=jnp.float32)
        * score_scale
    )
    scores = jnp.where(visible_mask(positions)[:, None], scores, MASKED)
    largest = jnp.max(scores, axis=-1, keepdims=True)
    exponent = jnp.exp(scores - largest)
    return exponent / jnp.sum(exponent, axis=-1, keepdims=True)


def forward_block(shared, values, positions, score_scale):
    weights = softmax_weights(shared, positions, score_scale).astype(jnp.bfloat16)
    return jnp.einsum(
        "nhqk,nkhd->nqhd", weights, values, preferred_element_type=jnp.float32
    ).astype(jnp.bfloat16)


def backward_block(shared, values, upstream, positions, score_scale):
    weights = softmax_weights(shared, positions, score_scale)
    rounded = weights.astype(jnp.bfloat16)
    output_b = jnp.einsum("nhqk,nkhd->nqhd", rounded, values, preferred_element_type=jnp.float32)
    row_delta = jnp.sum(upstream.astype(jnp.float32) * output_b, axis=-1)
    value_grad = jnp.einsum(
        "nhqk,nqhd->nkhd", rounded, upstream, preferred_element_type=jnp.float32
    ).astype(jnp.bfloat16)
    prob_grad = jnp.einsum("nqhd,nkhd->nhqk", upstream, values, preferred_element_type=jnp.float32)
    score_grad = (
        weights * (prob_grad - jnp.transpose(row_delta, (0, 2, 1))[..., None]) * score_scale
    ).astype(jnp.bfloat16)
    shared_grad = jnp.einsum(
        "nhqk,nkhd->nqhd", score_grad, shared, preferred_element_type=jnp.float32
    )
    shared_grad = shared_grad + jnp.einsum(
        "nhqk,nqhd->nkhd", score_grad, shared, preferred_element_type=jnp.float32
    )
    return (shared_grad.astype(jnp.bfloat16), value_grad)


def route_plan(slot_tokens, seq_index, range_here, seq_count, group_count, tok_dev, slot_count):
    block_rows = slot_tokens.shape[0] // seq_count
    source = slot_tokens // tok_dev
    local_row = (slot_tokens - range_here * tok_dev).reshape(seq_count, block_rows)
    owned_here = (source == range_here).reshape(seq_count, block_rows)
    slot_rank = jnp.cumsum(owned_here.astype(jnp.int32), axis=1) - 1
    selected = owned_here[:, None, :] & (
        slot_rank[:, None, :] == jnp.arange(slot_count)[None, :, None]
    )
    send_rows = jnp.sum(jnp.where(selected, local_row[:, None, :], 0), axis=2)
    filled = jnp.any(selected, axis=2)
    send = filled[:, :, None] & (send_rows[:, :, None] == jnp.arange(tok_dev)[None, None, :])
    block_order = lax.dynamic_slice_in_dim(slot_tokens, seq_index * block_rows, block_rows)
    block_source = block_order // tok_dev
    indicator = (block_source[:, None] == jnp.arange(group_count)[None, :]).astype(jnp.int32)
    block_rank = jnp.sum(jnp.cumsum(indicator, axis=0) * indicator, axis=1) - 1
    gather = (block_source[:, None, None] == jnp.arange(group_count)[None, :, None]) & (
        block_rank[:, None, None] == jnp.arange(slot_count)[None, None, :]
    )
    return (
        send.astype(jnp.bfloat16),
        gather.astype(jnp.bfloat16),
        block_order,
    )


def per_device(shared_fwd, values_fwd, shared_bwd, values_bwd, upstream_bwd, cluster_order):
    seq_count = lax.axis_size("seq")
    mp_count = lax.axis_size("mp")
    seq_index = lax.axis_index("seq")
    mp_index = lax.axis_index("mp")
    tok_dev = shared_fwd.shape[1]
    features = shared_fwd.shape[2]
    group_features = features // mp_count
    heads_dev = group_features // HEAD_DIM
    group_count = seq_count * mp_count
    range_here = seq_index * mp_count + mp_index
    block_rows = cluster_order.shape[2] // seq_count
    slot_count = 2 * block_rows // group_count
    score_scale = 1.0 / math.sqrt(HEAD_DIM)
    axes = ("seq", "mp")
    plan_fwd = route_plan(
        cluster_order[0, 0], seq_index, range_here, seq_count, group_count, tok_dev, slot_count
    )
    plan_bwd = route_plan(
        cluster_order[0, 1], seq_index, range_here, seq_count, group_count, tok_dev, slot_count
    )

    def exchange(arrays, send):
        packed = [
            jnp.einsum(
                "skt,tmf->smkf",
                send,
                array[0].reshape(tok_dev, mp_count, group_features),
                preferred_element_type=jnp.bfloat16,
            )
            for array in arrays
        ]
        stacked = jnp.stack(packed, axis=2).reshape(
            group_count, len(arrays), slot_count, group_features
        )
        return lax.all_to_all(stacked, axes, split_axis=0, concat_axis=0, tiled=True)

    def gather_block(arrived, gather):
        rows = jnp.einsum("irk,rakf->aif", gather, arrived, preferred_element_type=jnp.bfloat16)
        return [row.reshape(1, block_rows, heads_dev, HEAD_DIM) for row in rows]

    def give_back(results, gather, send):
        flat = jnp.stack([r.reshape(block_rows, group_features) for r in results], axis=0)
        placed = jnp.einsum("irk,aif->rakf", gather, flat, preferred_element_type=jnp.bfloat16)
        arrived = lax.all_to_all(placed, axes, split_axis=0, concat_axis=0, tiled=True)
        arrived = arrived.reshape(seq_count, mp_count, len(results), slot_count, group_features)
        rows = jnp.einsum("skt,smakf->atmf", send, arrived, preferred_element_type=jnp.bfloat16)
        return [row.reshape(1, tok_dev, features) for row in rows]

    positions_f = plan_fwd[2].reshape(-1, CLUSTER)
    positions_b = plan_bwd[2].reshape(-1, CLUSTER)
    arrived_b = exchange((shared_bwd, values_bwd, upstream_bwd), plan_bwd[0])
    arrived_b, shared_fwd, values_fwd = lax.optimization_barrier((arrived_b, shared_fwd, values_fwd))
    arrived_f = exchange((shared_fwd, values_fwd), plan_fwd[0])
    shared_b, values_b, upstream_b = gather_block(arrived_b, plan_bwd[1])
    shared_grad, value_grad = backward_block(shared_b, values_b, upstream_b, positions_b, score_scale)
    shared_grad, value_grad, arrived_f = lax.optimization_barrier((shared_grad, value_grad, arrived_f))
    shared_out, values_out = give_back((shared_grad, value_grad), plan_bwd[1], plan_bwd[0])
    shared_f, values_f = gather_block(arrived_f, plan_fwd[1])
    attended = forward_block(shared_f, values_f, positions_f, score_scale)
    attended, shared_out, values_out = lax.optimization_barrier((attended, shared_out, values_out))
    shared_grad_in, values_grad_in = shifted((shared_out, values_out), "pipe", -1)
    (forward_out,) = give_back((attended,), plan_fwd[1], plan_fwd[0])
    forward_in = shifted(forward_out, "pipe", 1)
    return (forward_in, shared_grad_in, values_grad_in)


def solution(mesh):
    in_specs = (
        P("pipe", ("seq", "mp"), None),
        P("pipe", ("seq", "mp"), None),
        P("pipe", ("seq", "mp"), None),
        P("pipe", ("seq", "mp"), None),
        P("pipe", ("seq", "mp"), None),
        P("pipe", None, None),
    )
    out_specs = (
        P("pipe", ("seq", "mp"), None),
        P("pipe", ("seq", "mp"), None),
        P("pipe", ("seq", "mp"), None),
    )
    return jax.shard_map(
        per_device, mesh=mesh, in_specs=in_specs, out_specs=out_specs, check_vma=False
    )
```

```python
import math

import jax
import jax.numpy as jnp
from jax import lax
from jax.sharding import PartitionSpec as P

HEAD_DIM = 128
CLUSTER = 256


MASKED = -1e30


def shifted(block, axis, distance):
    devices = range(lax.axis_size(axis))
    route = [(i - distance, i) for i in devices if i - distance in devices]
    return lax.ppermute(block, axis, route)


def visible_mask(positions):
    count = positions.shape[1]
    earlier = positions[:, None, :] < positions[:, :, None]
    earliest = positions == jnp.min(positions, axis=1, keepdims=True)
    diagonal = (jnp.arange(count)[:, None] == jnp.arange(count)[None, :])[None]
    return earlier | diagonal & earliest[:, :, None]


def softmax_weights(shared, positions, score_scale):
    scores = (
        jnp.einsum("nqhd,nkhd->nhqk", shared, shared, preferred_element_type=jnp.float32)
        * score_scale
    )
    scores = jnp.where(visible_mask(positions)[:, None], scores, MASKED)
    largest = jnp.max(scores, axis=-1, keepdims=True)
    exponent = jnp.exp(scores - largest)
    return exponent / jnp.sum(exponent, axis=-1, keepdims=True)


def forward_block(shared, values, positions, score_scale):
    weights = softmax_weights(shared, positions, score_scale).astype(jnp.bfloat16)
    return jnp.einsum(
        "nhqk,nkhd->nqhd", weights, values, preferred_element_type=jnp.float32
    ).astype(jnp.bfloat16)


def backward_block(shared, values, upstream, positions, score_scale):
    weights = softmax_weights(shared, positions, score_scale)
    rounded = weights.astype(jnp.bfloat16)
    output_b = jnp.einsum("nhqk,nkhd->nqhd", rounded, values, preferred_element_type=jnp.float32)
    row_delta = jnp.sum(upstream.astype(jnp.float32) * output_b, axis=-1)
    value_grad = jnp.einsum(
        "nhqk,nqhd->nkhd", rounded, upstream, preferred_element_type=jnp.float32
    ).astype(jnp.bfloat16)
    prob_grad = jnp.einsum("nqhd,nkhd->nhqk", upstream, values, preferred_element_type=jnp.float32)
    score_grad = (
        weights * (prob_grad - jnp.transpose(row_delta, (0, 2, 1))[..., None]) * score_scale
    ).astype(jnp.bfloat16)
    shared_grad = jnp.einsum(
        "nhqk,nkhd->nqhd", score_grad, shared, preferred_element_type=jnp.float32
    )
    shared_grad = shared_grad + jnp.einsum(
        "nhqk,nqhd->nkhd", score_grad, shared, preferred_element_type=jnp.float32
    )
    return (shared_grad.astype(jnp.bfloat16), value_grad)


def route_plan(slot_tokens, seq_index, range_here, seq_count, group_count, tok_dev, slot_count):
    block_rows = slot_tokens.shape[0] // seq_count
    source = slot_tokens // tok_dev
    local_row = (slot_tokens - range_here * tok_dev).reshape(seq_count, block_rows)
    owned_here = (source == range_here).reshape(seq_count, block_rows)
    slot_rank = jnp.cumsum(owned_here.astype(jnp.int32), axis=1) - 1
    selected = owned_here[:, None, :] & (
        slot_rank[:, None, :] == jnp.arange(slot_count)[None, :, None]
    )
    send_rows = jnp.sum(jnp.where(selected, local_row[:, None, :], 0), axis=2)
    filled = jnp.any(selected, axis=2)
    send = filled[:, :, None] & (send_rows[:, :, None] == jnp.arange(tok_dev)[None, None, :])
    block_order = lax.dynamic_slice_in_dim(slot_tokens, seq_index * block_rows, block_rows)
    block_source = block_order // tok_dev
    indicator = (block_source[:, None] == jnp.arange(group_count)[None, :]).astype(jnp.int32)
    block_rank = jnp.sum(jnp.cumsum(indicator, axis=0) * indicator, axis=1) - 1
    gather = (block_source[:, None, None] == jnp.arange(group_count)[None, :, None]) & (
        block_rank[:, None, None] == jnp.arange(slot_count)[None, None, :]
    )
    return (
        send.astype(jnp.bfloat16),
        gather.astype(jnp.bfloat16),
        block_order,
    )


def per_device(shared_fwd, values_fwd, shared_bwd, values_bwd, upstream_bwd, cluster_order):
    seq_count = lax.axis_size("seq")
    mp_count = lax.axis_size("mp")
    seq_index = lax.axis_index("seq")
    mp_index = lax.axis_index("mp")
    tok_dev = shared_fwd.shape[1]
    features = shared_fwd.shape[2]
    group_features = features // mp_count
    heads_dev = group_features // HEAD_DIM
    group_count = seq_count * mp_count
    range_here = seq_index * mp_count + mp_index
    block_rows = cluster_order.shape[2] // seq_count
    slot_count = 2 * block_rows // group_count
    score_scale = 1.0 / math.sqrt(HEAD_DIM)
    axes = ("seq", "mp")
    plan_fwd = route_plan(
        cluster_order[0, 0], seq_index, range_here, seq_count, group_count, tok_dev, slot_count
    )
    plan_bwd = route_plan(
        cluster_order[0, 1], seq_index, range_here, seq_count, group_count, tok_dev, slot_count
    )

    def exchange(arrays, send):
        packed = [
            jnp.einsum(
                "skt,tmf->smkf",
                send[index],
                array[0].reshape(tok_dev, mp_count, group_features),
                preferred_element_type=jnp.bfloat16,
            )
            for index, array in enumerate(arrays)
        ]
        stacked = jnp.stack(packed, axis=2).reshape(
            group_count, len(arrays), slot_count, group_features
        )
        return lax.all_to_all(stacked, axes, split_axis=0, concat_axis=0, tiled=True)

    def gather_block(arrived, gather):
        rows = jnp.einsum("irk,rakf->aif", gather, arrived, preferred_element_type=jnp.bfloat16)
        return [row.reshape(1, block_rows, heads_dev, HEAD_DIM) for row in rows]

    def give_back(results, gather, send):
        flat = jnp.stack([r.reshape(block_rows, group_features) for r in results], axis=0)
        placed = jnp.einsum("airk,aif->rakf", gather, flat, preferred_element_type=jnp.bfloat16)
        arrived = lax.all_to_all(placed, axes, split_axis=0, concat_axis=0, tiled=True)
        arrived = arrived.reshape(seq_count, mp_count, len(results), slot_count, group_features)
        rows = jnp.einsum("askt,smakf->atmf", send, arrived, preferred_element_type=jnp.bfloat16)
        return [row.reshape(1, tok_dev, features) for row in rows]

    positions_f = plan_fwd[2].reshape(-1, CLUSTER)
    positions_b = plan_bwd[2].reshape(-1, CLUSTER)
    arrived = exchange(
        (shared_bwd, values_bwd, upstream_bwd, shared_fwd, values_fwd),
        jnp.stack([plan_bwd[0]] * 3 + [plan_fwd[0]] * 2),
    )
    shared_b, values_b, upstream_b = gather_block(arrived[:, :3], plan_bwd[1])
    shared_grad, value_grad = backward_block(shared_b, values_b, upstream_b, positions_b, score_scale)
    shared_f, values_f = gather_block(arrived[:, 3:], plan_fwd[1])
    attended = forward_block(shared_f, values_f, positions_f, score_scale)
    shared_out, values_out, forward_out = give_back(
        (shared_grad, value_grad, attended),
        jnp.stack([plan_bwd[1]] * 2 + [plan_fwd[1]]),
        jnp.stack([plan_bwd[0]] * 2 + [plan_fwd[0]]),
    )
    shared_grad_in, values_grad_in = shifted((shared_out, values_out), "pipe", -1)
    forward_in = shifted(forward_out, "pipe", 1)
    return (forward_in, shared_grad_in, values_grad_in)


def solution(mesh):
    in_specs = (
        P("pipe", ("seq", "mp"), None),
        P("pipe", ("seq", "mp"), None),
        P("pipe", ("seq", "mp"), None),
        P("pipe", ("seq", "mp"), None),
        P("pipe", ("seq", "mp"), None),
        P("pipe", None, None),
    )
    out_specs = (
        P("pipe", ("seq", "mp"), None),
        P("pipe", ("seq", "mp"), None),
        P("pipe", ("seq", "mp"), None),
    )
    return jax.shard_map(
        per_device, mesh=mesh, in_specs=in_specs, out_specs=out_specs, check_vma=False
    )
```

```python
import math

import jax
import jax.numpy as jnp
from jax import lax
from jax.sharding import PartitionSpec as P

HEAD_DIM = 128
CLUSTER = 256


MASKED = -1e30


def shifted(block, axis, distance):
    devices = range(lax.axis_size(axis))
    route = [(i - distance, i) for i in devices if i - distance in devices]
    return lax.ppermute(block, axis, route)


def visible_mask(positions):
    count = positions.shape[1]
    earlier = positions[:, None, :] < positions[:, :, None]
    earliest = positions == jnp.min(positions, axis=1, keepdims=True)
    diagonal = (jnp.arange(count)[:, None] == jnp.arange(count)[None, :])[None]
    return earlier | diagonal & earliest[:, :, None]


def softmax_weights(shared, positions, score_scale):
    scores = (
        jnp.einsum("nqhd,nkhd->nhqk", shared, shared, preferred_element_type=jnp.float32)
        * score_scale
    )
    scores = jnp.where(visible_mask(positions)[:, None], scores, MASKED)
    largest = jnp.max(scores, axis=-1, keepdims=True)
    exponent = jnp.exp(scores - largest)
    return exponent / jnp.sum(exponent, axis=-1, keepdims=True)


def forward_block(shared, values, positions, score_scale):
    weights = softmax_weights(shared, positions, score_scale).astype(jnp.bfloat16)
    return jnp.einsum(
        "nhqk,nkhd->nqhd", weights, values, preferred_element_type=jnp.float32
    ).astype(jnp.bfloat16)


def backward_block(shared, values, upstream, positions, score_scale):
    weights = softmax_weights(shared, positions, score_scale)
    rounded = weights.astype(jnp.bfloat16)
    output_b = jnp.einsum("nhqk,nkhd->nqhd", rounded, values, preferred_element_type=jnp.float32)
    row_delta = jnp.sum(upstream.astype(jnp.float32) * output_b, axis=-1)
    value_grad = jnp.einsum(
        "nhqk,nqhd->nkhd", rounded, upstream, preferred_element_type=jnp.float32
    ).astype(jnp.bfloat16)
    prob_grad = jnp.einsum("nqhd,nkhd->nhqk", upstream, values, preferred_element_type=jnp.float32)
    score_grad = (
        weights * (prob_grad - jnp.transpose(row_delta, (0, 2, 1))[..., None]) * score_scale
    ).astype(jnp.bfloat16)
    shared_grad = jnp.einsum(
        "nhqk,nkhd->nqhd", score_grad, shared, preferred_element_type=jnp.float32
    )
    shared_grad = shared_grad + jnp.einsum(
        "nhqk,nqhd->nkhd", score_grad, shared, preferred_element_type=jnp.float32
    )
    return (shared_grad.astype(jnp.bfloat16), value_grad)


def route_plan(slot_tokens, seq_index, range_here, seq_count, group_count, tok_dev, slot_count):
    block_rows = slot_tokens.shape[0] // seq_count
    source = slot_tokens // tok_dev
    local_row = (slot_tokens - range_here * tok_dev).reshape(seq_count, block_rows)
    owned_here = (source == range_here).reshape(seq_count, block_rows)
    slot_rank = jnp.cumsum(owned_here.astype(jnp.int32), axis=1) - 1
    selected = owned_here[:, None, :] & (
        slot_rank[:, None, :] == jnp.arange(slot_count)[None, :, None]
    )
    send_rows = jnp.sum(jnp.where(selected, local_row[:, None, :], 0), axis=2)
    filled = jnp.any(selected, axis=2)
    send = filled[:, :, None] & (send_rows[:, :, None] == jnp.arange(tok_dev)[None, None, :])
    block_order = lax.dynamic_slice_in_dim(slot_tokens, seq_index * block_rows, block_rows)
    block_source = block_order // tok_dev
    indicator = (block_source[:, None] == jnp.arange(group_count)[None, :]).astype(jnp.int32)
    block_rank = jnp.sum(jnp.cumsum(indicator, axis=0) * indicator, axis=1) - 1
    gather = (block_source[:, None, None] == jnp.arange(group_count)[None, :, None]) & (
        block_rank[:, None, None] == jnp.arange(slot_count)[None, None, :]
    )
    return (
        send.astype(jnp.bfloat16),
        gather.astype(jnp.bfloat16),
        block_order,
    )


def per_device(shared_fwd, values_fwd, shared_bwd, values_bwd, upstream_bwd, cluster_order):
    seq_count = lax.axis_size("seq")
    mp_count = lax.axis_size("mp")
    seq_index = lax.axis_index("seq")
    mp_index = lax.axis_index("mp")
    tok_dev = shared_fwd.shape[1]
    features = shared_fwd.shape[2]
    group_features = features // mp_count
    heads_dev = group_features // HEAD_DIM
    group_count = seq_count * mp_count
    range_here = seq_index * mp_count + mp_index
    block_rows = cluster_order.shape[2] // seq_count
    slot_count = 2 * block_rows // group_count
    score_scale = 1.0 / math.sqrt(HEAD_DIM)
    axes = ("seq", "mp")
    order_fwd = cluster_order[0, 0]
    order_bwd = cluster_order[0, 1]
    order_prev_fwd = shifted(order_fwd, "pipe", 1)
    order_next_bwd = shifted(order_bwd, "pipe", -1)

    def plan(order):
        return route_plan(order, seq_index, range_here, seq_count, group_count, tok_dev, slot_count)

    own_f, own_b = plan(order_fwd), plan(order_bwd)
    back_f, back_b = plan(order_prev_fwd), plan(order_next_bwd)

    def exchange(arrays, send):
        packed = [
            jnp.einsum(
                "skt,tmf->smkf",
                send[index],
                array[0].reshape(tok_dev, mp_count, group_features),
                preferred_element_type=jnp.bfloat16,
            )
            for index, array in enumerate(arrays)
        ]
        stacked = jnp.stack(packed, axis=2).reshape(
            group_count, len(arrays), slot_count, group_features
        )
        return lax.all_to_all(stacked, axes, split_axis=0, concat_axis=0, tiled=True)

    def give_back(results, gather, send):
        placed = jnp.einsum("airk,aif->rakf", gather, results, preferred_element_type=jnp.bfloat16)
        arrived = lax.all_to_all(placed, axes, split_axis=0, concat_axis=0, tiled=True)
        arrived = arrived.reshape(seq_count, mp_count, results.shape[0], slot_count, group_features)
        rows = jnp.einsum("askt,smakf->atmf", send, arrived, preferred_element_type=jnp.bfloat16)
        return [row.reshape(1, tok_dev, features) for row in rows]

    positions_f = own_f[2].reshape(-1, CLUSTER)
    positions_b = own_b[2].reshape(-1, CLUSTER)
    send_in = jnp.stack([own_b[0]] * 3 + [own_f[0]] * 2)
    gather_in = jnp.stack([own_b[1]] * 3 + [own_f[1]] * 2)
    arrived = exchange((shared_bwd, values_bwd, upstream_bwd, shared_fwd, values_fwd), send_in)
    rows = jnp.einsum("airk,rakf->aif", gather_in, arrived, preferred_element_type=jnp.bfloat16)
    rows = rows.reshape(5, 1, block_rows, heads_dev, HEAD_DIM)
    shared_grad, value_grad = backward_block(rows[0], rows[1], rows[2], positions_b, score_scale)
    moved_b = shifted(
        jnp.stack([shared_grad, value_grad]).reshape(2, block_rows, group_features), "pipe", -1
    )
    attended = forward_block(rows[3], rows[4], positions_f, score_scale)
    moved_f = shifted(attended.reshape(1, block_rows, group_features), "pipe", 1)
    shared_grad_in, values_grad_in, forward_in = give_back(
        jnp.concatenate([moved_b, moved_f]),
        jnp.stack([back_b[1]] * 2 + [back_f[1]]),
        jnp.stack([back_b[0]] * 2 + [back_f[0]]),
    )
    return (forward_in, shared_grad_in, values_grad_in)


def solution(mesh):
    in_specs = (
        P("pipe", ("seq", "mp"), None),
        P("pipe", ("seq", "mp"), None),
        P("pipe", ("seq", "mp"), None),
        P("pipe", ("seq", "mp"), None),
        P("pipe", ("seq", "mp"), None),
        P("pipe", None, None),
    )
    out_specs = (
        P("pipe", ("seq", "mp"), None),
        P("pipe", ("seq", "mp"), None),
        P("pipe", ("seq", "mp"), None),
    )
    return jax.shard_map(
        per_device, mesh=mesh, in_specs=in_specs, out_specs=out_specs, check_vma=False
    )
```

```python
import math

import jax
import jax.numpy as jnp
from jax import lax
from jax.sharding import PartitionSpec as P

HEAD_DIM = 128
CLUSTER = 256


MASKED = -1e30


def shifted(block, axis, distance):
    devices = range(lax.axis_size(axis))
    route = [(i - distance, i) for i in devices if i - distance in devices]
    return lax.ppermute(block, axis, route)


def visible_mask(positions):
    count = positions.shape[1]
    earlier = positions[:, None, :] < positions[:, :, None]
    earliest = positions == jnp.min(positions, axis=1, keepdims=True)
    diagonal = (jnp.arange(count)[:, None] == jnp.arange(count)[None, :])[None]
    return earlier | diagonal & earliest[:, :, None]


def softmax_weights(shared, positions, score_scale):
    scores = (
        jnp.einsum("nqhd,nkhd->nhqk", shared, shared, preferred_element_type=jnp.float32)
        * score_scale
    )
    scores = jnp.where(visible_mask(positions)[:, None], scores, MASKED)
    largest = jnp.max(scores, axis=-1, keepdims=True)
    exponent = jnp.exp(scores - largest)
    return exponent / jnp.sum(exponent, axis=-1, keepdims=True)


def forward_block(shared, values, positions, score_scale):
    weights = softmax_weights(shared, positions, score_scale).astype(jnp.bfloat16)
    return jnp.einsum(
        "nhqk,nkhd->nqhd", weights, values, preferred_element_type=jnp.float32
    ).astype(jnp.bfloat16)


def backward_block(shared, values, upstream, positions, score_scale):
    weights = softmax_weights(shared, positions, score_scale)
    rounded = weights.astype(jnp.bfloat16)
    output_b = jnp.einsum("nhqk,nkhd->nqhd", rounded, values, preferred_element_type=jnp.float32)
    row_delta = jnp.sum(upstream.astype(jnp.float32) * output_b, axis=-1)
    value_grad = jnp.einsum(
        "nhqk,nqhd->nkhd", rounded, upstream, preferred_element_type=jnp.float32
    ).astype(jnp.bfloat16)
    prob_grad = jnp.einsum("nqhd,nkhd->nhqk", upstream, values, preferred_element_type=jnp.float32)
    score_grad = (
        weights * (prob_grad - jnp.transpose(row_delta, (0, 2, 1))[..., None]) * score_scale
    ).astype(jnp.bfloat16)
    shared_grad = jnp.einsum(
        "nhqk,nkhd->nqhd", score_grad, shared, preferred_element_type=jnp.float32
    )
    shared_grad = shared_grad + jnp.einsum(
        "nhqk,nqhd->nkhd", score_grad, shared, preferred_element_type=jnp.float32
    )
    return (shared_grad.astype(jnp.bfloat16), value_grad)


def route_plan(slot_tokens, seq_index, range_here, seq_count, group_count, tok_dev, slot_count):
    block_rows = slot_tokens.shape[0] // seq_count
    source = slot_tokens // tok_dev
    local_row = (slot_tokens - range_here * tok_dev).reshape(seq_count, block_rows)
    owned_here = (source == range_here).reshape(seq_count, block_rows)
    slot_rank = jnp.cumsum(owned_here.astype(jnp.int32), axis=1) - 1
    selected = owned_here[:, None, :] & (
        slot_rank[:, None, :] == jnp.arange(slot_count)[None, :, None]
    )
    send_rows = jnp.sum(jnp.where(selected, local_row[:, None, :], 0), axis=2)
    filled = jnp.any(selected, axis=2)
    send = filled[:, :, None] & (send_rows[:, :, None] == jnp.arange(tok_dev)[None, None, :])
    block_order = lax.dynamic_slice_in_dim(slot_tokens, seq_index * block_rows, block_rows)
    block_source = block_order // tok_dev
    indicator = (block_source[:, None] == jnp.arange(group_count)[None, :]).astype(jnp.int32)
    block_rank = jnp.sum(jnp.cumsum(indicator, axis=0) * indicator, axis=1) - 1
    gather = (block_source[:, None, None] == jnp.arange(group_count)[None, :, None]) & (
        block_rank[:, None, None] == jnp.arange(slot_count)[None, None, :]
    )
    return (
        send.astype(jnp.bfloat16),
        gather.astype(jnp.bfloat16),
        block_order,
    )


def unit_plan(slot_tokens, seq_index, range_here, seq_count, group_count, tok_dev):
    block_rows = slot_tokens.shape[0] // seq_count
    unit = 8
    source = (slot_tokens // tok_dev).reshape(seq_count, block_rows)
    member = (source[:, :, None] == jnp.arange(group_count)[None, None, :]).astype(jnp.int32)
    before = jnp.cumsum(member, axis=1) - member
    slot_rank = jnp.sum(before * member, axis=2)
    second = slot_rank // unit
    place = slot_rank % unit
    units = jnp.sum(member, axis=1) // unit
    empty = (units == 0).astype(jnp.int32)
    double = (units == 2).astype(jnp.int32)
    empty_rank = jnp.cumsum(empty, axis=0) - empty
    double_rank = jnp.cumsum(double, axis=0) - double
    match = (
        (double[:, None, :] == 1)
        & (empty[None, :, :] == 1)
        & (double_rank[:, None, :] == empty_rank[None, :, :])
    ).astype(jnp.int32)
    blocks = jnp.arange(seq_count)
    carrier = jnp.sum(match * blocks[None, :, None], axis=1)
    owner = jnp.sum(match * blocks[:, None, None], axis=0)
    overfull = jnp.any(jnp.sum(empty, axis=1) > 1)
    block_of = jnp.broadcast_to(blocks[:, None], (seq_count, block_rows))
    mine = source == range_here
    carrier_slot = jnp.sum(member * carrier[:, None, :], axis=2)
    target = jnp.where(second == 0, block_of, carrier_slot)
    code = jnp.where(mine, target * unit + place, -1).reshape(-1)
    local = (slot_tokens - range_here * tok_dev)
    token_hit = (local[:, None] == jnp.arange(tok_dev)[None, :]) & mine.reshape(-1)[:, None]
    token_code = jnp.sum(jnp.where(token_hit, code[:, None], 0), axis=0)
    send = (token_code[None, :] == jnp.arange(seq_count * unit)[:, None]).reshape(
        seq_count, unit, tok_dev
    )
    src_here = lax.dynamic_index_in_dim(source, seq_index, keepdims=False)
    second_here = lax.dynamic_index_in_dim(second, seq_index, keepdims=False)
    place_here = lax.dynamic_index_in_dim(place, seq_index, keepdims=False)
    carrier_rows = lax.dynamic_index_in_dim(carrier_slot, seq_index, keepdims=False)
    empty_here = lax.dynamic_index_in_dim(empty, seq_index, keepdims=False)
    owner_here = lax.dynamic_index_in_dim(owner, seq_index, keepdims=False)
    at_place = place_here[:, None] == jnp.arange(unit)[None, :]
    first_pick = (
        (second_here == 0)[:, None, None]
        & (src_here[:, None, None] == jnp.arange(group_count)[None, :, None])
        & at_place[:, None, :]
    )
    second_pick = (
        (second_here == 1)[:, None, None]
        & (carrier_rows[:, None, None] == blocks[None, :, None])
        & at_place[:, None, :]
    )
    foreign = empty_here == 1
    spare = ((second_here == 1)[None, :] & at_place.T)
    relay = foreign[:, None] & (owner_here[:, None] == blocks[None, :])
    bf = jnp.bfloat16
    return dict(
        send=send.astype(bf),
        first=first_pick.astype(bf),
        second=second_pick.astype(bf),
        foreign=foreign.astype(bf),
        spare=spare.astype(bf),
        relay=relay.astype(bf),
        overfull=overfull,
    )


def per_device(shared_fwd, values_fwd, shared_bwd, values_bwd, upstream_bwd, cluster_order):
    seq_count = lax.axis_size("seq")
    mp_count = lax.axis_size("mp")
    seq_index = lax.axis_index("seq")
    mp_index = lax.axis_index("mp")
    tok_dev = shared_fwd.shape[1]
    features = shared_fwd.shape[2]
    group_features = features // mp_count
    heads_dev = group_features // HEAD_DIM
    group_count = seq_count * mp_count
    range_here = seq_index * mp_count + mp_index
    block_rows = cluster_order.shape[2] // seq_count
    slot_count = 2 * block_rows // group_count
    unit = slot_count // 2
    score_scale = 1.0 / math.sqrt(HEAD_DIM)
    axes = ("seq", "mp")
    order_fwd = cluster_order[0, 0]
    order_bwd = cluster_order[0, 1]
    order_prev_fwd = shifted(order_fwd, "pipe", 1)
    order_next_bwd = shifted(order_bwd, "pipe", -1)

    def plan(order):
        return route_plan(order, seq_index, range_here, seq_count, group_count, tok_dev, slot_count)

    def uplan(order):
        return unit_plan(order, seq_index, range_here, seq_count, group_count, tok_dev)

    own_f, own_b = plan(order_fwd), plan(order_bwd)
    back_f, back_b = plan(order_prev_fwd), plan(order_next_bwd)
    uown_f, uown_b = uplan(order_fwd), uplan(order_bwd)
    uback_f, uback_b = uplan(order_prev_fwd), uplan(order_next_bwd)
    overfull = (uown_f["overfull"] | uown_b["overfull"]).astype(jnp.int32)
    fast = lax.psum(overfull, "pipe") == 0

    def stacked(plans, key, counts):
        return jnp.stack([p[key] for p, n in zip(plans, counts) for _ in range(n)])

    inputs = (shared_bwd, values_bwd, upstream_bwd, shared_fwd, values_fwd)

    def pack(arrays, send, rows):
        packed = [
            jnp.einsum(
                "skt,tmf->smkf",
                send[index],
                array[0].reshape(tok_dev, mp_count, group_features),
                preferred_element_type=jnp.bfloat16,
            )
            for index, array in enumerate(arrays)
        ]
        return jnp.stack(packed, axis=2).reshape(group_count, len(arrays), rows, group_features)

    def padded_in(arrays):
        send = stacked((own_b, own_f), 0, (3, 2))
        gather = stacked((own_b, own_f), 1, (3, 2))
        arrived = lax.all_to_all(
            pack(arrays, send, slot_count), axes, split_axis=0, concat_axis=0, tiled=True
        )
        return jnp.einsum("airk,rakf->aif", gather, arrived, preferred_element_type=jnp.bfloat16)

    def unit_in(arrays):
        plans = (uown_b, uown_f)
        counts = (3, 2)
        arrived = lax.all_to_all(
            pack(arrays, stacked(plans, "send", counts), unit),
            axes, split_axis=0, concat_axis=0, tiled=True,
        )
        spare = jnp.einsum(
            "ar,rapf->apf", stacked(plans, "foreign", counts), arrived,
            preferred_element_type=jnp.bfloat16,
        )
        spares = lax.all_gather(spare, "seq", axis=0, tiled=False)
        first = jnp.einsum(
            "airp,rapf->aif", stacked(plans, "first", counts), arrived,
            preferred_element_type=jnp.float32,
        )
        second = jnp.einsum(
            "aibp,bapf->aif", stacked(plans, "second", counts), spares,
            preferred_element_type=jnp.float32,
        )
        return (first + second).astype(jnp.bfloat16)

    def padded_out(results):
        gather = stacked((back_b, back_f), 1, (2, 1))
        send = stacked((back_b, back_f), 0, (2, 1))
        placed = jnp.einsum("airk,aif->rakf", gather, results, preferred_element_type=jnp.bfloat16)
        arrived = lax.all_to_all(placed, axes, split_axis=0, concat_axis=0, tiled=True)
        arrived = arrived.reshape(seq_count, mp_count, results.shape[0], slot_count, group_features)
        return jnp.einsum("askt,smakf->atmf", send, arrived, preferred_element_type=jnp.bfloat16)

    def unit_out(results):
        plans = (uback_b, uback_f)
        counts = (2, 1)
        spare = jnp.einsum(
            "api,aif->apf", stacked(plans, "spare", counts), results,
            preferred_element_type=jnp.bfloat16,
        )
        spares = lax.all_gather(spare, "seq", axis=0, tiled=False)
        first = jnp.einsum(
            "airp,aif->rapf", stacked(plans, "first", counts), results,
            preferred_element_type=jnp.float32,
        )
        relayed = jnp.einsum(
            "arb,bapf->rapf", stacked(plans, "relay", counts), spares,
            preferred_element_type=jnp.float32,
        )
        placed = (first + relayed).astype(jnp.bfloat16)
        arrived = lax.all_to_all(placed, axes, split_axis=0, concat_axis=0, tiled=True)
        arrived = arrived.reshape(seq_count, mp_count, results.shape[0], unit, group_features)
        return jnp.einsum(
            "adpt,dmapf->atmf", stacked(plans, "send", counts), arrived,
            preferred_element_type=jnp.bfloat16,
        )

    positions_f = own_f[2].reshape(-1, CLUSTER)
    positions_b = own_b[2].reshape(-1, CLUSTER)
    rows = lax.cond(fast, unit_in, padded_in, inputs)
    rows = rows.reshape(5, 1, block_rows, heads_dev, HEAD_DIM)
    shared_grad, value_grad = backward_block(rows[0], rows[1], rows[2], positions_b, score_scale)
    moved_b = shifted(
        jnp.stack([shared_grad, value_grad]).reshape(2, block_rows, group_features), "pipe", -1
    )
    attended = forward_block(rows[3], rows[4], positions_f, score_scale)
    moved_f = shifted(attended.reshape(1, block_rows, group_features), "pipe", 1)
    outs = lax.cond(fast, unit_out, padded_out, jnp.concatenate([moved_b, moved_f]))
    outs = [row.reshape(1, tok_dev, features) for row in outs]
    return (outs[2], outs[0], outs[1])


def solution(mesh):
    in_specs = (
        P("pipe", ("seq", "mp"), None),
        P("pipe", ("seq", "mp"), None),
        P("pipe", ("seq", "mp"), None),
        P("pipe", ("seq", "mp"), None),
        P("pipe", ("seq", "mp"), None),
        P("pipe", None, None),
    )
    out_specs = (
        P("pipe", ("seq", "mp"), None),
        P("pipe", ("seq", "mp"), None),
        P("pipe", ("seq", "mp"), None),
    )
    return jax.shard_map(
        per_device, mesh=mesh, in_specs=in_specs, out_specs=out_specs, check_vma=False
    )
```

```python
import math

import jax
import jax.numpy as jnp
from jax import lax
from jax.sharding import PartitionSpec as P

HEAD_DIM = 128
CLUSTER = 256


MASKED = -1e30


def shifted(block, axis, distance):
    devices = range(lax.axis_size(axis))
    route = [(i - distance, i) for i in devices if i - distance in devices]
    return lax.ppermute(block, axis, route)


def visible_mask(positions):
    count = positions.shape[1]
    earlier = positions[:, None, :] < positions[:, :, None]
    earliest = positions == jnp.min(positions, axis=1, keepdims=True)
    diagonal = (jnp.arange(count)[:, None] == jnp.arange(count)[None, :])[None]
    return earlier | diagonal & earliest[:, :, None]


def softmax_weights(shared, positions, score_scale):
    scores = (
        jnp.einsum("nqhd,nkhd->nhqk", shared, shared, preferred_element_type=jnp.float32)
        * score_scale
    )
    scores = jnp.where(visible_mask(positions)[:, None], scores, MASKED)
    largest = jnp.max(scores, axis=-1, keepdims=True)
    exponent = jnp.exp(scores - largest)
    return exponent / jnp.sum(exponent, axis=-1, keepdims=True)


def forward_block(shared, values, positions, score_scale):
    weights = softmax_weights(shared, positions, score_scale).astype(jnp.bfloat16)
    return jnp.einsum(
        "nhqk,nkhd->nqhd", weights, values, preferred_element_type=jnp.float32
    ).astype(jnp.bfloat16)


def backward_block(shared, values, upstream, positions, score_scale):
    weights = softmax_weights(shared, positions, score_scale)
    rounded = weights.astype(jnp.bfloat16)
    output_b = jnp.einsum("nhqk,nkhd->nqhd", rounded, values, preferred_element_type=jnp.float32)
    row_delta = jnp.sum(upstream.astype(jnp.float32) * output_b, axis=-1)
    value_grad = jnp.einsum(
        "nhqk,nqhd->nkhd", rounded, upstream, preferred_element_type=jnp.float32
    ).astype(jnp.bfloat16)
    prob_grad = jnp.einsum("nqhd,nkhd->nhqk", upstream, values, preferred_element_type=jnp.float32)
    score_grad = (
        weights * (prob_grad - jnp.transpose(row_delta, (0, 2, 1))[..., None]) * score_scale
    ).astype(jnp.bfloat16)
    shared_grad = jnp.einsum(
        "nhqk,nkhd->nqhd", score_grad, shared, preferred_element_type=jnp.float32
    )
    shared_grad = shared_grad + jnp.einsum(
        "nhqk,nqhd->nkhd", score_grad, shared, preferred_element_type=jnp.float32
    )
    return (shared_grad.astype(jnp.bfloat16), value_grad)


def route_plan(slot_tokens, seq_index, range_here, seq_count, group_count, tok_dev, slot_count):
    block_rows = slot_tokens.shape[0] // seq_count
    source = slot_tokens // tok_dev
    local_row = (slot_tokens - range_here * tok_dev).reshape(seq_count, block_rows)
    owned_here = (source == range_here).reshape(seq_count, block_rows)
    slot_rank = jnp.cumsum(owned_here.astype(jnp.int32), axis=1) - 1
    selected = owned_here[:, None, :] & (
        slot_rank[:, None, :] == jnp.arange(slot_count)[None, :, None]
    )
    send_rows = jnp.sum(jnp.where(selected, local_row[:, None, :], 0), axis=2)
    filled = jnp.any(selected, axis=2)
    send = filled[:, :, None] & (send_rows[:, :, None] == jnp.arange(tok_dev)[None, None, :])
    block_order = lax.dynamic_slice_in_dim(slot_tokens, seq_index * block_rows, block_rows)
    block_source = block_order // tok_dev
    indicator = (block_source[:, None] == jnp.arange(group_count)[None, :]).astype(jnp.int32)
    block_rank = jnp.sum(jnp.cumsum(indicator, axis=0) * indicator, axis=1) - 1
    gather = (block_source[:, None, None] == jnp.arange(group_count)[None, :, None]) & (
        block_rank[:, None, None] == jnp.arange(slot_count)[None, None, :]
    )
    return (
        send.astype(jnp.bfloat16),
        gather.astype(jnp.bfloat16),
        block_order,
    )


def unit_plan(slot_tokens, seq_index, range_here, seq_count, group_count, tok_dev):
    block_rows = slot_tokens.shape[0] // seq_count
    unit = 8
    source = (slot_tokens // tok_dev).reshape(seq_count, block_rows)
    member = (source[:, :, None] == jnp.arange(group_count)[None, None, :]).astype(jnp.int32)
    earlier = (jnp.arange(block_rows)[None, :] < jnp.arange(block_rows)[:, None]).astype(jnp.bfloat16)
    before = jnp.einsum(
        "ij,bjr->bir", earlier, member.astype(jnp.bfloat16), preferred_element_type=jnp.float32
    ).astype(jnp.int32)
    slot_rank = jnp.sum(before * member, axis=2)
    second = slot_rank // unit
    place = slot_rank % unit
    units = jnp.sum(member, axis=1) // unit
    empty = (units == 0).astype(jnp.int32)
    double = (units == 2).astype(jnp.int32)
    empty_rank = jnp.cumsum(empty, axis=0) - empty
    double_rank = jnp.cumsum(double, axis=0) - double
    match = (
        (double[:, None, :] == 1)
        & (empty[None, :, :] == 1)
        & (double_rank[:, None, :] == empty_rank[None, :, :])
    ).astype(jnp.int32)
    blocks = jnp.arange(seq_count)
    carrier = jnp.sum(match * blocks[None, :, None], axis=1)
    owner = jnp.sum(match * blocks[:, None, None], axis=0)
    overfull = jnp.any(jnp.sum(empty, axis=1) > 1)
    block_of = jnp.broadcast_to(blocks[:, None], (seq_count, block_rows))
    mine = source == range_here
    carrier_slot = jnp.sum(member * carrier[:, None, :], axis=2)
    target = jnp.where(second == 0, block_of, carrier_slot)
    code = jnp.where(mine, target * unit + place, -1).reshape(-1)
    local = (slot_tokens - range_here * tok_dev)
    token_hit = (local[:, None] == jnp.arange(tok_dev)[None, :]) & mine.reshape(-1)[:, None]
    token_code = jnp.sum(jnp.where(token_hit, code[:, None], 0), axis=0)
    send = (token_code[None, :] == jnp.arange(seq_count * unit)[:, None]).reshape(
        seq_count, unit, tok_dev
    )
    src_here = lax.dynamic_index_in_dim(source, seq_index, keepdims=False)
    second_here = lax.dynamic_index_in_dim(second, seq_index, keepdims=False)
    place_here = lax.dynamic_index_in_dim(place, seq_index, keepdims=False)
    carrier_rows = lax.dynamic_index_in_dim(carrier_slot, seq_index, keepdims=False)
    empty_here = lax.dynamic_index_in_dim(empty, seq_index, keepdims=False)
    owner_here = lax.dynamic_index_in_dim(owner, seq_index, keepdims=False)
    at_place = place_here[:, None] == jnp.arange(unit)[None, :]
    first_pick = (
        (second_here == 0)[:, None, None]
        & (src_here[:, None, None] == jnp.arange(group_count)[None, :, None])
        & at_place[:, None, :]
    )
    second_pick = (
        (second_here == 1)[:, None, None]
        & (carrier_rows[:, None, None] == blocks[None, :, None])
        & at_place[:, None, :]
    )
    foreign = empty_here == 1
    spare = ((second_here == 1)[None, :] & at_place.T)
    relay = foreign[:, None] & (owner_here[:, None] == blocks[None, :])
    bf = jnp.bfloat16
    return dict(
        send=send.astype(bf),
        first=first_pick.astype(bf),
        second=second_pick.astype(bf),
        foreign=foreign.astype(bf),
        spare=spare.astype(bf),
        relay=relay.astype(bf),
        overfull=overfull,
    )


def per_device(shared_fwd, values_fwd, shared_bwd, values_bwd, upstream_bwd, cluster_order):
    seq_count = lax.axis_size("seq")
    mp_count = lax.axis_size("mp")
    seq_index = lax.axis_index("seq")
    mp_index = lax.axis_index("mp")
    tok_dev = shared_fwd.shape[1]
    features = shared_fwd.shape[2]
    group_features = features // mp_count
    heads_dev = group_features // HEAD_DIM
    group_count = seq_count * mp_count
    range_here = seq_index * mp_count + mp_index
    block_rows = cluster_order.shape[2] // seq_count
    slot_count = 2 * block_rows // group_count
    unit = slot_count // 2
    score_scale = 1.0 / math.sqrt(HEAD_DIM)
    axes = ("seq", "mp")
    order_fwd = cluster_order[0, 0]
    order_bwd = cluster_order[0, 1]
    order_prev_fwd = shifted(order_fwd, "pipe", 1)
    order_next_bwd = shifted(order_bwd, "pipe", -1)

    def plan(order):
        return route_plan(order, seq_index, range_here, seq_count, group_count, tok_dev, slot_count)

    def uplan(order):
        return unit_plan(order, seq_index, range_here, seq_count, group_count, tok_dev)

    def overfull(order):
        source = (order // tok_dev).reshape(seq_count, block_rows)
        member = source[:, :, None] == jnp.arange(group_count)[None, None, :]
        units = jnp.sum(member.astype(jnp.int32), axis=1) // (slot_count // 2)
        return jnp.any(jnp.sum((units == 0).astype(jnp.int32), axis=1) > 1)

    fast_in = ~(overfull(order_fwd) | overfull(order_bwd))
    fast_out = ~(overfull(order_prev_fwd) | overfull(order_next_bwd))

    def stacked(plans, key, counts):
        return jnp.stack([p[key] for p, n in zip(plans, counts) for _ in range(n)])

    inputs = (shared_bwd, values_bwd, upstream_bwd, shared_fwd, values_fwd)

    def pack(arrays, send, rows):
        packed = [
            jnp.einsum(
                "skt,tmf->smkf",
                send[index],
                array[0].reshape(tok_dev, mp_count, group_features),
                preferred_element_type=jnp.bfloat16,
            )
            for index, array in enumerate(arrays)
        ]
        return jnp.stack(packed, axis=2).reshape(group_count, len(arrays), rows, group_features)

    def padded_in(arrays):
        own_f, own_b = plan(order_fwd), plan(order_bwd)
        send = stacked((own_b, own_f), 0, (3, 2))
        gather = stacked((own_b, own_f), 1, (3, 2))
        arrived = lax.all_to_all(
            pack(arrays, send, slot_count), axes, split_axis=0, concat_axis=0, tiled=True
        )
        return jnp.einsum("airk,rakf->aif", gather, arrived, preferred_element_type=jnp.bfloat16)

    def unit_in(arrays):
        plans = (uplan(order_bwd), uplan(order_fwd))
        counts = (3, 2)
        arrived = lax.all_to_all(
            pack(arrays, stacked(plans, "send", counts), unit),
            axes, split_axis=0, concat_axis=0, tiled=True,
        )
        spare = jnp.einsum(
            "ar,rapf->apf", stacked(plans, "foreign", counts), arrived,
            preferred_element_type=jnp.bfloat16,
        )
        spares = lax.all_gather(spare, "seq", axis=0, tiled=False)
        first = jnp.einsum(
            "airp,rapf->aif", stacked(plans, "first", counts), arrived,
            preferred_element_type=jnp.float32,
        )
        second = jnp.einsum(
            "aibp,bapf->aif", stacked(plans, "second", counts), spares,
            preferred_element_type=jnp.float32,
        )
        return (first + second).astype(jnp.bfloat16)

    def padded_out(results):
        back_f, back_b = plan(order_prev_fwd), plan(order_next_bwd)
        gather = stacked((back_b, back_f), 1, (2, 1))
        send = stacked((back_b, back_f), 0, (2, 1))
        placed = jnp.einsum("airk,aif->rakf", gather, results, preferred_element_type=jnp.bfloat16)
        arrived = lax.all_to_all(placed, axes, split_axis=0, concat_axis=0, tiled=True)
        arrived = arrived.reshape(seq_count, mp_count, results.shape[0], slot_count, group_features)
        return jnp.einsum("askt,smakf->atmf", send, arrived, preferred_element_type=jnp.bfloat16)

    def unit_out(results):
        plans = (uplan(order_next_bwd), uplan(order_prev_fwd))
        counts = (2, 1)
        spare = jnp.einsum(
            "api,aif->apf", stacked(plans, "spare", counts), results,
            preferred_element_type=jnp.bfloat16,
        )
        spares = lax.all_gather(spare, "seq", axis=0, tiled=False)
        first = jnp.einsum(
            "airp,aif->rapf", stacked(plans, "first", counts), results,
            preferred_element_type=jnp.float32,
        )
        relayed = jnp.einsum(
            "arb,bapf->rapf", stacked(plans, "relay", counts), spares,
            preferred_element_type=jnp.float32,
        )
        placed = (first + relayed).astype(jnp.bfloat16)
        arrived = lax.all_to_all(placed, axes, split_axis=0, concat_axis=0, tiled=True)
        arrived = arrived.reshape(seq_count, mp_count, results.shape[0], unit, group_features)
        return jnp.einsum(
            "adpt,dmapf->atmf", stacked(plans, "send", counts), arrived,
            preferred_element_type=jnp.bfloat16,
        )

    positions_f = lax.dynamic_slice_in_dim(order_fwd, seq_index * block_rows, block_rows)[None]
    positions_b = lax.dynamic_slice_in_dim(order_bwd, seq_index * block_rows, block_rows)[None]
    rows = lax.cond(fast_in, unit_in, padded_in, inputs)
    rows = rows.reshape(5, 1, block_rows, heads_dev, HEAD_DIM)
    shared_grad, value_grad = backward_block(rows[0], rows[1], rows[2], positions_b, score_scale)
    moved_b = shifted(
        jnp.stack([shared_grad, value_grad]).reshape(2, block_rows, group_features), "pipe", -1
    )
    attended = forward_block(rows[3], rows[4], positions_f, score_scale)
    moved_f = shifted(attended.reshape(1, block_rows, group_features), "pipe", 1)
    outs = lax.cond(fast_out, unit_out, padded_out, jnp.concatenate([moved_b, moved_f]))
    outs = [row.reshape(1, tok_dev, features) for row in outs]
    return (outs[2], outs[0], outs[1])


def solution(mesh):
    in_specs = (
        P("pipe", ("seq", "mp"), None),
        P("pipe", ("seq", "mp"), None),
        P("pipe", ("seq", "mp"), None),
        P("pipe", ("seq", "mp"), None),
        P("pipe", ("seq", "mp"), None),
        P("pipe", None, None),
    )
    out_specs = (
        P("pipe", ("seq", "mp"), None),
        P("pipe", ("seq", "mp"), None),
        P("pipe", ("seq", "mp"), None),
    )
    return jax.shard_map(
        per_device, mesh=mesh, in_specs=in_specs, out_specs=out_specs, check_vma=False
    )
```

```python
import math

import jax
import jax.numpy as jnp
from jax import lax
from jax.sharding import PartitionSpec as P

HEAD_DIM = 128
CLUSTER = 256


MASKED = -1e30


def shifted(block, axis, distance):
    devices = range(lax.axis_size(axis))
    route = [(i - distance, i) for i in devices if i - distance in devices]
    return lax.ppermute(block, axis, route)


def visible_mask(positions):
    count = positions.shape[1]
    earlier = positions[:, None, :] < positions[:, :, None]
    earliest = positions == jnp.min(positions, axis=1, keepdims=True)
    diagonal = (jnp.arange(count)[:, None] == jnp.arange(count)[None, :])[None]
    return earlier | diagonal & earliest[:, :, None]


def softmax_weights(shared, positions, score_scale):
    scores = (
        jnp.einsum("nqhd,nkhd->nhqk", shared, shared, preferred_element_type=jnp.float32)
        * score_scale
    )
    scores = jnp.where(visible_mask(positions)[:, None], scores, MASKED)
    largest = jnp.max(scores, axis=-1, keepdims=True)
    exponent = jnp.exp(scores - largest)
    return exponent / jnp.sum(exponent, axis=-1, keepdims=True)


def forward_block(shared, values, positions, score_scale):
    weights = softmax_weights(shared, positions, score_scale).astype(jnp.bfloat16)
    return jnp.einsum(
        "nhqk,nkhd->nqhd", weights, values, preferred_element_type=jnp.float32
    ).astype(jnp.bfloat16)


def backward_block(shared, values, upstream, positions, score_scale):
    weights = softmax_weights(shared, positions, score_scale)
    rounded = weights.astype(jnp.bfloat16)
    output_b = jnp.einsum("nhqk,nkhd->nqhd", rounded, values, preferred_element_type=jnp.float32)
    row_delta = jnp.sum(upstream.astype(jnp.float32) * output_b, axis=-1)
    value_grad = jnp.einsum(
        "nhqk,nqhd->nkhd", rounded, upstream, preferred_element_type=jnp.float32
    ).astype(jnp.bfloat16)
    prob_grad = jnp.einsum("nqhd,nkhd->nhqk", upstream, values, preferred_element_type=jnp.float32)
    score_grad = (
        weights * (prob_grad - jnp.transpose(row_delta, (0, 2, 1))[..., None]) * score_scale
    ).astype(jnp.bfloat16)
    shared_grad = jnp.einsum(
        "nhqk,nkhd->nqhd", score_grad, shared, preferred_element_type=jnp.float32
    )
    shared_grad = shared_grad + jnp.einsum(
        "nhqk,nqhd->nkhd", score_grad, shared, preferred_element_type=jnp.float32
    )
    return (shared_grad.astype(jnp.bfloat16), value_grad)


def route_plan(slot_tokens, seq_index, range_here, seq_count, group_count, tok_dev, slot_count):
    block_rows = slot_tokens.shape[0] // seq_count
    source = slot_tokens // tok_dev
    local_row = (slot_tokens - range_here * tok_dev).reshape(seq_count, block_rows)
    owned_here = (source == range_here).reshape(seq_count, block_rows)
    slot_rank = jnp.cumsum(owned_here.astype(jnp.int32), axis=1) - 1
    selected = owned_here[:, None, :] & (
        slot_rank[:, None, :] == jnp.arange(slot_count)[None, :, None]
    )
    send_rows = jnp.sum(jnp.where(selected, local_row[:, None, :], 0), axis=2)
    filled = jnp.any(selected, axis=2)
    send = filled[:, :, None] & (send_rows[:, :, None] == jnp.arange(tok_dev)[None, None, :])
    block_order = lax.dynamic_slice_in_dim(slot_tokens, seq_index * block_rows, block_rows)
    block_source = block_order // tok_dev
    indicator = (block_source[:, None] == jnp.arange(group_count)[None, :]).astype(jnp.int32)
    block_rank = jnp.sum(jnp.cumsum(indicator, axis=0) * indicator, axis=1) - 1
    gather = (block_source[:, None, None] == jnp.arange(group_count)[None, :, None]) & (
        block_rank[:, None, None] == jnp.arange(slot_count)[None, None, :]
    )
    return (
        send.astype(jnp.bfloat16),
        gather.astype(jnp.bfloat16),
        block_order,
    )


def unit_plan(slot_tokens, seq_index, range_here, seq_count, group_count, tok_dev):
    block_rows = slot_tokens.shape[0] // seq_count
    unit = 8
    source = (slot_tokens // tok_dev).reshape(seq_count, block_rows)
    member = (source[:, :, None] == jnp.arange(group_count)[None, None, :]).astype(jnp.int32)
    earlier = (jnp.arange(block_rows)[None, :] < jnp.arange(block_rows)[:, None]).astype(jnp.bfloat16)
    before = jnp.einsum(
        "ij,bjr->bir", earlier, member.astype(jnp.bfloat16), preferred_element_type=jnp.float32
    ).astype(jnp.int32)
    slot_rank = jnp.sum(before * member, axis=2)
    second = slot_rank // unit
    place = slot_rank % unit
    units = jnp.sum(member, axis=1) // unit
    empty = (units == 0).astype(jnp.int32)
    double = (units == 2).astype(jnp.int32)
    empty_rank = jnp.cumsum(empty, axis=0) - empty
    double_rank = jnp.cumsum(double, axis=0) - double
    match = (
        (double[:, None, :] == 1)
        & (empty[None, :, :] == 1)
        & (double_rank[:, None, :] == empty_rank[None, :, :])
    ).astype(jnp.int32)
    blocks = jnp.arange(seq_count)
    carrier = jnp.sum(match * blocks[None, :, None], axis=1)
    owner = jnp.sum(match * blocks[:, None, None], axis=0)
    overfull = jnp.any(jnp.sum(empty, axis=1) > 1)
    block_of = jnp.broadcast_to(blocks[:, None], (seq_count, block_rows))
    mine = source == range_here
    carrier_slot = jnp.sum(member * carrier[:, None, :], axis=2)
    target = jnp.where(second == 0, block_of, carrier_slot)
    code = jnp.where(mine, target * unit + place, -1).reshape(-1)
    local = (slot_tokens - range_here * tok_dev)
    token_hit = (local[:, None] == jnp.arange(tok_dev)[None, :]) & mine.reshape(-1)[:, None]
    token_code = jnp.sum(jnp.where(token_hit, code[:, None], 0), axis=0)
    send = (token_code[None, :] == jnp.arange(seq_count * unit)[:, None]).reshape(
        seq_count, unit, tok_dev
    )
    src_here = lax.dynamic_index_in_dim(source, seq_index, keepdims=False)
    second_here = lax.dynamic_index_in_dim(second, seq_index, keepdims=False)
    place_here = lax.dynamic_index_in_dim(place, seq_index, keepdims=False)
    carrier_rows = lax.dynamic_index_in_dim(carrier_slot, seq_index, keepdims=False)
    empty_here = lax.dynamic_index_in_dim(empty, seq_index, keepdims=False)
    owner_here = lax.dynamic_index_in_dim(owner, seq_index, keepdims=False)
    at_place = place_here[:, None] == jnp.arange(unit)[None, :]
    first_pick = (
        (second_here == 0)[:, None, None]
        & (src_here[:, None, None] == jnp.arange(group_count)[None, :, None])
        & at_place[:, None, :]
    )
    second_pick = (
        (second_here == 1)[:, None, None]
        & (carrier_rows[:, None, None] == blocks[None, :, None])
        & at_place[:, None, :]
    )
    foreign = empty_here == 1
    spare = ((second_here == 1)[None, :] & at_place.T)
    relay = foreign[:, None] & (owner_here[:, None] == blocks[None, :])
    forward_to = jnp.sum(relay.astype(jnp.int32) * blocks[None, :])
    double_here = lax.dynamic_index_in_dim(double, seq_index, keepdims=False)
    carrier_here = lax.dynamic_index_in_dim(carrier, seq_index, keepdims=False)
    return_to = jnp.sum(double_here * carrier_here)
    has_foreign = jnp.any(foreign)
    has_spare = jnp.any(double_here == 1)
    to_owner = (blocks == forward_to) & has_foreign
    to_carrier = (blocks == return_to) & has_spare
    bf = jnp.bfloat16
    return dict(
        send=send.astype(bf),
        first=first_pick.astype(bf),
        second=second_pick.astype(bf),
        foreign=foreign.astype(bf),
        spare=spare.astype(bf),
        relay=relay.astype(bf),
        to_owner=to_owner.astype(bf),
        to_carrier=to_carrier.astype(bf),
        overfull=overfull,
    )


def per_device(shared_fwd, values_fwd, shared_bwd, values_bwd, upstream_bwd, cluster_order):
    seq_count = lax.axis_size("seq")
    mp_count = lax.axis_size("mp")
    seq_index = lax.axis_index("seq")
    mp_index = lax.axis_index("mp")
    tok_dev = shared_fwd.shape[1]
    features = shared_fwd.shape[2]
    group_features = features // mp_count
    heads_dev = group_features // HEAD_DIM
    group_count = seq_count * mp_count
    range_here = seq_index * mp_count + mp_index
    block_rows = cluster_order.shape[2] // seq_count
    slot_count = 2 * block_rows // group_count
    unit = slot_count // 2
    score_scale = 1.0 / math.sqrt(HEAD_DIM)
    axes = ("seq", "mp")
    order_fwd = cluster_order[0, 0]
    order_bwd = cluster_order[0, 1]
    order_prev_fwd = shifted(order_fwd, "pipe", 1)
    order_next_bwd = shifted(order_bwd, "pipe", -1)

    def plan(order):
        return route_plan(order, seq_index, range_here, seq_count, group_count, tok_dev, slot_count)

    def uplan(order):
        return unit_plan(order, seq_index, range_here, seq_count, group_count, tok_dev)

    def overfull(order):
        source = (order // tok_dev).reshape(seq_count, block_rows)
        member = source[:, :, None] == jnp.arange(group_count)[None, None, :]
        units = jnp.sum(member.astype(jnp.int32), axis=1) // (slot_count // 2)
        return jnp.any(jnp.sum((units == 0).astype(jnp.int32), axis=1) > 1)

    fast_in = ~(overfull(order_fwd) | overfull(order_bwd))
    pipe_index = lax.axis_index("pipe")
    first_plane = pipe_index == 0
    last_plane = pipe_index == lax.axis_size("pipe") - 1
    fast_out = ~((overfull(order_prev_fwd) & ~first_plane) | (overfull(order_next_bwd) & ~last_plane))

    def stacked(plans, key, counts):
        return jnp.stack([p[key] for p, n in zip(plans, counts) for _ in range(n)])

    inputs = (shared_bwd, values_bwd, upstream_bwd, shared_fwd, values_fwd)

    def pack(arrays, send, rows):
        packed = [
            jnp.einsum(
                "skt,tmf->smkf",
                send[index],
                array[0].reshape(tok_dev, mp_count, group_features),
                preferred_element_type=jnp.bfloat16,
            )
            for index, array in enumerate(arrays)
        ]
        return jnp.stack(packed, axis=2).reshape(group_count, len(arrays), rows, group_features)

    def padded_in(arrays):
        own_f, own_b = plan(order_fwd), plan(order_bwd)
        send = stacked((own_b, own_f), 0, (3, 2))
        gather = stacked((own_b, own_f), 1, (3, 2))
        arrived = lax.all_to_all(
            pack(arrays, send, slot_count), axes, split_axis=0, concat_axis=0, tiled=True
        )
        return jnp.einsum("airk,rakf->aif", gather, arrived, preferred_element_type=jnp.bfloat16)

    def unit_in(arrays):
        plans = (uplan(order_bwd), uplan(order_fwd))
        counts = (3, 2)
        arrived = lax.all_to_all(
            pack(arrays, stacked(plans, "send", counts), unit),
            axes, split_axis=0, concat_axis=0, tiled=True,
        )
        spare = jnp.einsum(
            "ar,rapf->apf", stacked(plans, "foreign", counts), arrived,
            preferred_element_type=jnp.bfloat16,
        )
        spare = jnp.einsum(
            "ab,apf->bapf", stacked(plans, "to_owner", counts), spare,
            preferred_element_type=jnp.bfloat16,
        )
        spares = lax.all_to_all(spare, "seq", split_axis=0, concat_axis=0, tiled=True)
        first = jnp.einsum(
            "airp,rapf->aif", stacked(plans, "first", counts), arrived,
            preferred_element_type=jnp.float32,
        )
        second = jnp.einsum(
            "aibp,bapf->aif", stacked(plans, "second", counts), spares,
            preferred_element_type=jnp.float32,
        )
        return (first + second).astype(jnp.bfloat16)

    def padded_out(results):
        back_f, back_b = plan(order_prev_fwd), plan(order_next_bwd)
        gather = stacked((back_b, back_f), 1, (2, 1))
        send = stacked((back_b, back_f), 0, (2, 1))
        placed = jnp.einsum("airk,aif->rakf", gather, results, preferred_element_type=jnp.bfloat16)
        arrived = lax.all_to_all(placed, axes, split_axis=0, concat_axis=0, tiled=True)
        arrived = arrived.reshape(seq_count, mp_count, results.shape[0], slot_count, group_features)
        return jnp.einsum("askt,smakf->atmf", send, arrived, preferred_element_type=jnp.bfloat16)

    def unit_out(results):
        plans = (uplan(order_next_bwd), uplan(order_prev_fwd))
        counts = (2, 1)
        spare = jnp.einsum(
            "api,aif->apf", stacked(plans, "spare", counts), results,
            preferred_element_type=jnp.bfloat16,
        )
        spare = jnp.einsum(
            "ab,apf->bapf", stacked(plans, "to_carrier", counts), spare,
            preferred_element_type=jnp.bfloat16,
        )
        spares = lax.all_to_all(spare, "seq", split_axis=0, concat_axis=0, tiled=True)
        first = jnp.einsum(
            "airp,aif->rapf", stacked(plans, "first", counts), results,
            preferred_element_type=jnp.float32,
        )
        relayed = jnp.einsum(
            "arb,bapf->rapf", stacked(plans, "relay", counts), spares,
            preferred_element_type=jnp.float32,
        )
        placed = (first + relayed).astype(jnp.bfloat16)
        arrived = lax.all_to_all(placed, axes, split_axis=0, concat_axis=0, tiled=True)
        arrived = arrived.reshape(seq_count, mp_count, results.shape[0], unit, group_features)
        return jnp.einsum(
            "adpt,dmapf->atmf", stacked(plans, "send", counts), arrived,
            preferred_element_type=jnp.bfloat16,
        )

    positions_f = lax.dynamic_slice_in_dim(order_fwd, seq_index * block_rows, block_rows)[None]
    positions_b = lax.dynamic_slice_in_dim(order_bwd, seq_index * block_rows, block_rows)[None]
    rows = lax.cond(fast_in, unit_in, padded_in, inputs)
    rows = rows.reshape(5, 1, block_rows, heads_dev, HEAD_DIM)
    shared_grad, value_grad = backward_block(rows[0], rows[1], rows[2], positions_b, score_scale)
    moved_b = shifted(
        jnp.stack([shared_grad, value_grad]).reshape(2, block_rows, group_features), "pipe", -1
    )
    moved_b, rows_f = lax.optimization_barrier((moved_b, rows[3:]))
    attended = forward_block(rows_f[0], rows_f[1], positions_f, score_scale)
    moved_f = shifted(attended.reshape(1, block_rows, group_features), "pipe", 1)
    outs = lax.cond(fast_out, unit_out, padded_out, jnp.concatenate([moved_b, moved_f]))
    outs = [row.reshape(1, tok_dev, features) for row in outs]
    return (outs[2], outs[0], outs[1])


def solution(mesh):
    in_specs = (
        P("pipe", ("seq", "mp"), None),
        P("pipe", ("seq", "mp"), None),
        P("pipe", ("seq", "mp"), None),
        P("pipe", ("seq", "mp"), None),
        P("pipe", ("seq", "mp"), None),
        P("pipe", None, None),
    )
    out_specs = (
        P("pipe", ("seq", "mp"), None),
        P("pipe", ("seq", "mp"), None),
        P("pipe", ("seq", "mp"), None),
    )
    return jax.shard_map(
        per_device, mesh=mesh, in_specs=in_specs, out_specs=out_specs, check_vma=False
    )
```

```python
import math

import jax
import jax.numpy as jnp
from jax import lax
from jax.sharding import PartitionSpec as P

HEAD_DIM = 128
CLUSTER = 256


MASKED = -1e30


def shifted(block, axis, distance):
    devices = range(lax.axis_size(axis))
    route = [(i - distance, i) for i in devices if i - distance in devices]
    return lax.ppermute(block, axis, route)


def visible_mask(positions):
    count = positions.shape[1]
    earlier = positions[:, None, :] < positions[:, :, None]
    earliest = positions == jnp.min(positions, axis=1, keepdims=True)
    diagonal = (jnp.arange(count)[:, None] == jnp.arange(count)[None, :])[None]
    return earlier | diagonal & earliest[:, :, None]


def softmax_weights(shared, positions, score_scale):
    scores = (
        jnp.einsum("nqhd,nkhd->nhqk", shared, shared, preferred_element_type=jnp.float32)
        * score_scale
    )
    scores = jnp.where(visible_mask(positions)[:, None], scores, MASKED)
    largest = jnp.max(scores, axis=-1, keepdims=True)
    exponent = jnp.exp(scores - largest)
    return exponent / jnp.sum(exponent, axis=-1, keepdims=True)


def forward_block(shared, values, positions, score_scale):
    weights = softmax_weights(shared, positions, score_scale).astype(jnp.bfloat16)
    return jnp.einsum(
        "nhqk,nkhd->nqhd", weights, values, preferred_element_type=jnp.float32
    ).astype(jnp.bfloat16)


def backward_block(shared, values, upstream, positions, score_scale):
    weights = softmax_weights(shared, positions, score_scale)
    rounded = weights.astype(jnp.bfloat16)
    output_b = jnp.einsum("nhqk,nkhd->nqhd", rounded, values, preferred_element_type=jnp.float32)
    row_delta = jnp.sum(upstream.astype(jnp.float32) * output_b, axis=-1)
    value_grad = jnp.einsum(
        "nhqk,nqhd->nkhd", rounded, upstream, preferred_element_type=jnp.float32
    ).astype(jnp.bfloat16)
    prob_grad = jnp.einsum("nqhd,nkhd->nhqk", upstream, values, preferred_element_type=jnp.float32)
    score_grad = (
        weights * (prob_grad - jnp.transpose(row_delta, (0, 2, 1))[..., None]) * score_scale
    ).astype(jnp.bfloat16)
    shared_grad = jnp.einsum(
        "nhqk,nkhd->nqhd", score_grad, shared, preferred_element_type=jnp.float32
    )
    shared_grad = shared_grad + jnp.einsum(
        "nhqk,nqhd->nkhd", score_grad, shared, preferred_element_type=jnp.float32
    )
    return (shared_grad.astype(jnp.bfloat16), value_grad)


def route_plan(slot_tokens, seq_index, range_here, seq_count, group_count, tok_dev, slot_count):
    block_rows = slot_tokens.shape[0] // seq_count
    source = slot_tokens // tok_dev
    local_row = (slot_tokens - range_here * tok_dev).reshape(seq_count, block_rows)
    owned_here = (source == range_here).reshape(seq_count, block_rows)
    slot_rank = jnp.cumsum(owned_here.astype(jnp.int32), axis=1) - 1
    selected = owned_here[:, None, :] & (
        slot_rank[:, None, :] == jnp.arange(slot_count)[None, :, None]
    )
    send_rows = jnp.sum(jnp.where(selected, local_row[:, None, :], 0), axis=2)
    filled = jnp.any(selected, axis=2)
    send = filled[:, :, None] & (send_rows[:, :, None] == jnp.arange(tok_dev)[None, None, :])
    block_order = lax.dynamic_slice_in_dim(slot_tokens, seq_index * block_rows, block_rows)
    block_source = block_order // tok_dev
    indicator = (block_source[:, None] == jnp.arange(group_count)[None, :]).astype(jnp.int32)
    block_rank = jnp.sum(jnp.cumsum(indicator, axis=0) * indicator, axis=1) - 1
    gather = (block_source[:, None, None] == jnp.arange(group_count)[None, :, None]) & (
        block_rank[:, None, None] == jnp.arange(slot_count)[None, None, :]
    )
    return (
        send.astype(jnp.bfloat16),
        gather.astype(jnp.bfloat16),
        block_order,
    )


def per_device(shared_fwd, values_fwd, shared_bwd, values_bwd, upstream_bwd, cluster_order):
    seq_count = lax.axis_size("seq")
    mp_count = lax.axis_size("mp")
    seq_index = lax.axis_index("seq")
    mp_index = lax.axis_index("mp")
    tok_dev = shared_fwd.shape[1]
    features = shared_fwd.shape[2]
    group_features = features // mp_count
    heads_dev = group_features // HEAD_DIM
    group_count = seq_count * mp_count
    range_here = seq_index * mp_count + mp_index
    block_rows = cluster_order.shape[2] // seq_count
    slot_count = 2 * block_rows // group_count
    score_scale = 1.0 / math.sqrt(HEAD_DIM)
    axes = ("seq", "mp")
    pipe_index = lax.axis_index("pipe")
    last_plane = pipe_index == lax.axis_size("pipe") - 1
    order_fwd = cluster_order[0, 0]
    order_next_bwd, shared_bwd, values_bwd, upstream_bwd = shifted(
        (cluster_order[0, 1], shared_bwd, values_bwd, upstream_bwd), "pipe", -1
    )
    order_prev_fwd = shifted(order_fwd, "pipe", 1)

    def plan(order):
        return route_plan(order, seq_index, range_here, seq_count, group_count, tok_dev, slot_count)

    own_f, next_b, prev_f = plan(order_fwd), plan(order_next_bwd), plan(order_prev_fwd)

    def exchange(arrays, send):
        packed = [
            jnp.einsum(
                "skt,tmf->smkf",
                send,
                array[0].reshape(tok_dev, mp_count, group_features),
                preferred_element_type=jnp.bfloat16,
            )
            for array in arrays
        ]
        stacked = jnp.stack(packed, axis=2).reshape(
            group_count, len(arrays), slot_count, group_features
        )
        arrived = lax.all_to_all(stacked, axes, split_axis=0, concat_axis=0, tiled=True)
        return arrived

    def gather_block(arrived, gather):
        rows = jnp.einsum("irk,rakf->aif", gather, arrived, preferred_element_type=jnp.bfloat16)
        return rows.reshape(rows.shape[0], 1, block_rows, heads_dev, HEAD_DIM)

    def give_back(results, gather, send):
        placed = jnp.einsum("airk,aif->rakf", gather, results, preferred_element_type=jnp.bfloat16)
        arrived = lax.all_to_all(placed, axes, split_axis=0, concat_axis=0, tiled=True)
        arrived = arrived.reshape(seq_count, mp_count, results.shape[0], slot_count, group_features)
        rows = jnp.einsum("askt,smakf->atmf", send, arrived, preferred_element_type=jnp.bfloat16)
        return [row.reshape(1, tok_dev, features) for row in rows]

    arrived_f = exchange((shared_fwd, values_fwd), own_f[0])
    rows_f = gather_block(arrived_f, own_f[1])
    arrived_b = exchange((shared_bwd, values_bwd, upstream_bwd), next_b[0])
    attended = forward_block(rows_f[0], rows_f[1], own_f[2].reshape(-1, CLUSTER), score_scale)
    moved_f = shifted(attended.reshape(1, block_rows, group_features), "pipe", 1)
    rows_b = gather_block(arrived_b, next_b[1])
    shared_grad, value_grad = backward_block(
        rows_b[0], rows_b[1], rows_b[2], next_b[2].reshape(-1, CLUSTER), score_scale
    )
    results_b = jnp.stack([shared_grad, value_grad]).reshape(2, block_rows, group_features)
    results_b = jnp.where(last_plane, jnp.zeros_like(results_b), results_b)
    shared_grad_in, values_grad_in, forward_in = give_back(
        jnp.concatenate([results_b, moved_f]),
        jnp.stack([next_b[1]] * 2 + [prev_f[1]]),
        jnp.stack([next_b[0]] * 2 + [prev_f[0]]),
    )
    return (forward_in, shared_grad_in, values_grad_in)


def solution(mesh):
    in_specs = (
        P("pipe", ("seq", "mp"), None),
        P("pipe", ("seq", "mp"), None),
        P("pipe", ("seq", "mp"), None),
        P("pipe", ("seq", "mp"), None),
        P("pipe", ("seq", "mp"), None),
        P("pipe", None, None),
    )
    out_specs = (
        P("pipe", ("seq", "mp"), None),
        P("pipe", ("seq", "mp"), None),
        P("pipe", ("seq", "mp"), None),
    )
    return jax.shard_map(
        per_device, mesh=mesh, in_specs=in_specs, out_specs=out_specs, check_vma=False
    )
```

```python
import math

import jax
import jax.numpy as jnp
from jax import lax
from jax.sharding import PartitionSpec as P

HEAD_DIM = 128
CLUSTER = 256


MASKED = -1e30


def shifted(block, axis, distance):
    devices = range(lax.axis_size(axis))
    route = [(i - distance, i) for i in devices if i - distance in devices]
    return lax.ppermute(block, axis, route)


def visible_mask(positions):
    count = positions.shape[1]
    earlier = positions[:, None, :] < positions[:, :, None]
    earliest = positions == jnp.min(positions, axis=1, keepdims=True)
    diagonal = (jnp.arange(count)[:, None] == jnp.arange(count)[None, :])[None]
    return earlier | diagonal & earliest[:, :, None]


def softmax_weights(shared, positions, score_scale):
    scores = (
        jnp.einsum("nqhd,nkhd->nhqk", shared, shared, preferred_element_type=jnp.float32)
        * score_scale
    )
    scores = jnp.where(visible_mask(positions)[:, None], scores, MASKED)
    largest = jnp.max(scores, axis=-1, keepdims=True)
    exponent = jnp.exp(scores - largest)
    return exponent / jnp.sum(exponent, axis=-1, keepdims=True)


def forward_block(shared, values, positions, score_scale):
    weights = softmax_weights(shared, positions, score_scale).astype(jnp.bfloat16)
    return jnp.einsum(
        "nhqk,nkhd->nqhd", weights, values, preferred_element_type=jnp.float32
    ).astype(jnp.bfloat16)


def backward_block(shared, values, upstream, positions, score_scale):
    weights = softmax_weights(shared, positions, score_scale)
    rounded = weights.astype(jnp.bfloat16)
    output_b = jnp.einsum("nhqk,nkhd->nqhd", rounded, values, preferred_element_type=jnp.float32)
    row_delta = jnp.sum(upstream.astype(jnp.float32) * output_b, axis=-1)
    value_grad = jnp.einsum(
        "nhqk,nqhd->nkhd", rounded, upstream, preferred_element_type=jnp.float32
    ).astype(jnp.bfloat16)
    prob_grad = jnp.einsum("nqhd,nkhd->nhqk", upstream, values, preferred_element_type=jnp.float32)
    score_grad = (
        weights * (prob_grad - jnp.transpose(row_delta, (0, 2, 1))[..., None]) * score_scale
    ).astype(jnp.bfloat16)
    shared_grad = jnp.einsum(
        "nhqk,nkhd->nqhd", score_grad, shared, preferred_element_type=jnp.float32
    )
    shared_grad = shared_grad + jnp.einsum(
        "nhqk,nqhd->nkhd", score_grad, shared, preferred_element_type=jnp.float32
    )
    return (shared_grad.astype(jnp.bfloat16), value_grad)


def route_plan(slot_tokens, seq_index, range_here, seq_count, group_count, tok_dev, slot_count):
    block_rows = slot_tokens.shape[0] // seq_count
    source = slot_tokens // tok_dev
    local_row = (slot_tokens - range_here * tok_dev).reshape(seq_count, block_rows)
    owned_here = (source == range_here).reshape(seq_count, block_rows)
    slot_rank = jnp.cumsum(owned_here.astype(jnp.int32), axis=1) - 1
    selected = owned_here[:, None, :] & (
        slot_rank[:, None, :] == jnp.arange(slot_count)[None, :, None]
    )
    send_rows = jnp.sum(jnp.where(selected, local_row[:, None, :], 0), axis=2)
    filled = jnp.any(selected, axis=2)
    send = filled[:, :, None] & (send_rows[:, :, None] == jnp.arange(tok_dev)[None, None, :])
    block_order = lax.dynamic_slice_in_dim(slot_tokens, seq_index * block_rows, block_rows)
    block_source = block_order // tok_dev
    indicator = (block_source[:, None] == jnp.arange(group_count)[None, :]).astype(jnp.int32)
    block_rank = jnp.sum(jnp.cumsum(indicator, axis=0) * indicator, axis=1) - 1
    gather = (block_source[:, None, None] == jnp.arange(group_count)[None, :, None]) & (
        block_rank[:, None, None] == jnp.arange(slot_count)[None, None, :]
    )
    return (
        send.astype(jnp.bfloat16),
        gather.astype(jnp.bfloat16),
        block_order,
    )


def per_device(shared_fwd, values_fwd, shared_bwd, values_bwd, upstream_bwd, cluster_order):
    seq_count = lax.axis_size("seq")
    mp_count = lax.axis_size("mp")
    seq_index = lax.axis_index("seq")
    mp_index = lax.axis_index("mp")
    tok_dev = shared_fwd.shape[1]
    features = shared_fwd.shape[2]
    group_features = features // mp_count
    heads_dev = group_features // HEAD_DIM
    group_count = seq_count * mp_count
    range_here = seq_index * mp_count + mp_index
    block_rows = cluster_order.shape[2] // seq_count
    slot_count = 2 * block_rows // group_count
    score_scale = 1.0 / math.sqrt(HEAD_DIM)
    axes = ("seq", "mp")
    pipe_index = lax.axis_index("pipe")
    last_plane = pipe_index == lax.axis_size("pipe") - 1
    order_fwd = cluster_order[0, 0]
    order_next_bwd = shifted(cluster_order[0, 1], "pipe", -1)
    order_prev_fwd = shifted(order_fwd, "pipe", 1)

    def plan(order):
        return route_plan(order, seq_index, range_here, seq_count, group_count, tok_dev, slot_count)

    own_f, next_b, prev_f = plan(order_fwd), plan(order_next_bwd), plan(order_prev_fwd)

    def pack(arrays, send):
        packed = [
            jnp.einsum(
                "skt,tmf->smkf",
                send,
                array[0].reshape(tok_dev, mp_count, group_features),
                preferred_element_type=jnp.bfloat16,
            )
            for array in arrays
        ]
        return jnp.stack(packed, axis=2).reshape(
            group_count, len(arrays), slot_count, group_features
        )

    def exchange(packed):
        return lax.all_to_all(packed, axes, split_axis=0, concat_axis=0, tiled=True)

    def gather_block(arrived, gather):
        rows = jnp.einsum("irk,rakf->aif", gather, arrived, preferred_element_type=jnp.bfloat16)
        return rows.reshape(rows.shape[0], 1, block_rows, heads_dev, HEAD_DIM)

    def give_back(results, gather, send):
        placed = jnp.einsum("airk,aif->rakf", gather, results, preferred_element_type=jnp.bfloat16)
        arrived = lax.all_to_all(placed, axes, split_axis=0, concat_axis=0, tiled=True)
        arrived = arrived.reshape(seq_count, mp_count, results.shape[0], slot_count, group_features)
        return [
            jnp.einsum(
                "skt,smkf->tmf", send[index], arrived[:, :, index],
                preferred_element_type=jnp.bfloat16,
            ).reshape(1, tok_dev, features)
            for index in range(results.shape[0])
        ]

    packed_f = pack((shared_fwd, values_fwd), own_f[0])
    packed_f, inputs_b = lax.optimization_barrier(
        (packed_f, jnp.concatenate([shared_bwd, values_bwd, upstream_bwd]))
    )
    arrived_f = exchange(packed_f)
    inputs_b = shifted(inputs_b, "pipe", -1)
    shared_bwd, values_bwd, upstream_bwd = inputs_b[0:1], inputs_b[1:2], inputs_b[2:3]
    rows_f = gather_block(arrived_f, own_f[1])
    arrived_b = exchange(pack((shared_bwd, values_bwd, upstream_bwd), next_b[0]))
    attended = forward_block(rows_f[0], rows_f[1], own_f[2].reshape(-1, CLUSTER), score_scale)
    moved_f = shifted(attended.reshape(1, block_rows, group_features), "pipe", 1)
    rows_b = gather_block(arrived_b, next_b[1])
    shared_grad, value_grad = backward_block(
        rows_b[0], rows_b[1], rows_b[2], next_b[2].reshape(-1, CLUSTER), score_scale
    )
    results_b = jnp.stack([shared_grad, value_grad]).reshape(2, block_rows, group_features)
    results_b = jnp.where(last_plane, jnp.zeros_like(results_b), results_b)
    shared_grad_in, values_grad_in, forward_in = give_back(
        jnp.concatenate([results_b, moved_f]),
        jnp.stack([next_b[1]] * 2 + [prev_f[1]]),
        jnp.stack([next_b[0]] * 2 + [prev_f[0]]),
    )
    return (forward_in, shared_grad_in, values_grad_in)


def solution(mesh):
    in_specs = (
        P("pipe", ("seq", "mp"), None),
        P("pipe", ("seq", "mp"), None),
        P("pipe", ("seq", "mp"), None),
        P("pipe", ("seq", "mp"), None),
        P("pipe", ("seq", "mp"), None),
        P("pipe", None, None),
    )
    out_specs = (
        P("pipe", ("seq", "mp"), None),
        P("pipe", ("seq", "mp"), None),
        P("pipe", ("seq", "mp"), None),
    )
    return jax.shard_map(
        per_device, mesh=mesh, in_specs=in_specs, out_specs=out_specs, check_vma=False
    )
```

```python
import math

import jax
import jax.numpy as jnp
from jax import lax
from jax.sharding import PartitionSpec as P

HEAD_DIM = 128
CLUSTER = 256


MASKED = -1e30


def shifted(block, axis, distance):
    devices = range(lax.axis_size(axis))
    route = [(i - distance, i) for i in devices if i - distance in devices]
    return lax.ppermute(block, axis, route)


def visible_mask(positions):
    count = positions.shape[1]
    earlier = positions[:, None, :] < positions[:, :, None]
    earliest = positions == jnp.min(positions, axis=1, keepdims=True)
    diagonal = (jnp.arange(count)[:, None] == jnp.arange(count)[None, :])[None]
    return earlier | diagonal & earliest[:, :, None]


def softmax_weights(shared, positions, score_scale):
    scores = (
        jnp.einsum("nqhd,nkhd->nhqk", shared, shared, preferred_element_type=jnp.float32)
        * score_scale
    )
    scores = jnp.where(visible_mask(positions)[:, None], scores, MASKED)
    largest = jnp.max(scores, axis=-1, keepdims=True)
    exponent = jnp.exp(scores - largest)
    return exponent / jnp.sum(exponent, axis=-1, keepdims=True)


def forward_block(shared, values, positions, score_scale):
    weights = softmax_weights(shared, positions, score_scale).astype(jnp.bfloat16)
    return jnp.einsum(
        "nhqk,nkhd->nqhd", weights, values, preferred_element_type=jnp.float32
    ).astype(jnp.bfloat16)


def backward_block(shared, values, upstream, positions, score_scale):
    weights = softmax_weights(shared, positions, score_scale)
    rounded = weights.astype(jnp.bfloat16)
    output_b = jnp.einsum("nhqk,nkhd->nqhd", rounded, values, preferred_element_type=jnp.float32)
    row_delta = jnp.sum(upstream.astype(jnp.float32) * output_b, axis=-1)
    value_grad = jnp.einsum(
        "nhqk,nqhd->nkhd", rounded, upstream, preferred_element_type=jnp.float32
    ).astype(jnp.bfloat16)
    prob_grad = jnp.einsum("nqhd,nkhd->nhqk", upstream, values, preferred_element_type=jnp.float32)
    score_grad = (
        weights * (prob_grad - jnp.transpose(row_delta, (0, 2, 1))[..., None]) * score_scale
    ).astype(jnp.bfloat16)
    shared_grad = jnp.einsum(
        "nhqk,nkhd->nqhd", score_grad, shared, preferred_element_type=jnp.float32
    )
    shared_grad = shared_grad + jnp.einsum(
        "nhqk,nqhd->nkhd", score_grad, shared, preferred_element_type=jnp.float32
    )
    return (shared_grad.astype(jnp.bfloat16), value_grad)


def route_plan(slot_tokens, seq_index, range_here, seq_count, group_count, tok_dev, slot_count):
    block_rows = slot_tokens.shape[0] // seq_count
    source = slot_tokens // tok_dev
    local_row = (slot_tokens - range_here * tok_dev).reshape(seq_count, block_rows)
    owned_here = (source == range_here).reshape(seq_count, block_rows)
    slot_rank = jnp.cumsum(owned_here.astype(jnp.int32), axis=1) - 1
    selected = owned_here[:, None, :] & (
        slot_rank[:, None, :] == jnp.arange(slot_count)[None, :, None]
    )
    send_rows = jnp.sum(jnp.where(selected, local_row[:, None, :], 0), axis=2)
    filled = jnp.any(selected, axis=2)
    send = filled[:, :, None] & (send_rows[:, :, None] == jnp.arange(tok_dev)[None, None, :])
    block_order = lax.dynamic_slice_in_dim(slot_tokens, seq_index * block_rows, block_rows)
    block_source = block_order // tok_dev
    indicator = (block_source[:, None] == jnp.arange(group_count)[None, :]).astype(jnp.int32)
    block_rank = jnp.sum(jnp.cumsum(indicator, axis=0) * indicator, axis=1) - 1
    gather = (block_source[:, None, None] == jnp.arange(group_count)[None, :, None]) & (
        block_rank[:, None, None] == jnp.arange(slot_count)[None, None, :]
    )
    return (
        send.astype(jnp.bfloat16),
        gather.astype(jnp.bfloat16),
        block_order,
    )


def per_device(shared_fwd, values_fwd, shared_bwd, values_bwd, upstream_bwd, cluster_order):
    seq_count = lax.axis_size("seq")
    mp_count = lax.axis_size("mp")
    seq_index = lax.axis_index("seq")
    mp_index = lax.axis_index("mp")
    tok_dev = shared_fwd.shape[1]
    features = shared_fwd.shape[2]
    group_features = features // mp_count
    heads_dev = group_features // HEAD_DIM
    group_count = seq_count * mp_count
    range_here = seq_index * mp_count + mp_index
    block_rows = cluster_order.shape[2] // seq_count
    slot_count = 2 * block_rows // group_count
    score_scale = 1.0 / math.sqrt(HEAD_DIM)
    axes = ("seq", "mp")
    pipe_index = lax.axis_index("pipe")
    last_plane = pipe_index == lax.axis_size("pipe") - 1
    order_fwd = cluster_order[0, 0]
    order_next_bwd = shifted(cluster_order[0, 1], "pipe", -1)
    inputs_b = shifted(jnp.concatenate([shared_bwd, values_bwd, upstream_bwd]), "pipe", -1)
    shared_bwd, values_bwd, upstream_bwd = inputs_b[0:1], inputs_b[1:2], inputs_b[2:3]
    order_prev_fwd = shifted(order_fwd, "pipe", 1)

    def plan(order):
        return route_plan(order, seq_index, range_here, seq_count, group_count, tok_dev, slot_count)

    own_f, next_b, prev_f = plan(order_fwd), plan(order_next_bwd), plan(order_prev_fwd)

    def exchange(arrays, send):
        packed = [
            jnp.einsum("skt,tf->skf", send, array[0], preferred_element_type=jnp.bfloat16)
            for array in arrays
        ]
        stacked = jnp.stack(packed, axis=1).reshape(
            seq_count, len(arrays), slot_count, mp_count, group_features
        )
        stacked = jnp.transpose(stacked, (0, 3, 1, 2, 4)).reshape(
            group_count, len(arrays), slot_count, group_features
        )
        arrived = lax.all_to_all(stacked, axes, split_axis=0, concat_axis=0, tiled=True)
        return arrived

    def gather_block(arrived, gather):
        rows = jnp.einsum("irk,rakf->aif", gather, arrived, preferred_element_type=jnp.bfloat16)
        return rows.reshape(rows.shape[0], 1, block_rows, heads_dev, HEAD_DIM)

    def give_back(results, gather, send):
        placed = jnp.einsum("airk,aif->rakf", gather, results, preferred_element_type=jnp.bfloat16)
        arrived = lax.all_to_all(placed, axes, split_axis=0, concat_axis=0, tiled=True)
        arrived = arrived.reshape(seq_count, mp_count, results.shape[0], slot_count, group_features)
        rows = jnp.einsum("askt,smakf->atmf", send, arrived, preferred_element_type=jnp.bfloat16)
        return [row.reshape(1, tok_dev, features) for row in rows]

    arrived_f = exchange((shared_fwd, values_fwd), own_f[0])
    rows_f = gather_block(arrived_f, own_f[1])
    arrived_b = exchange((shared_bwd, values_bwd, upstream_bwd), next_b[0])
    attended = forward_block(rows_f[0], rows_f[1], own_f[2].reshape(-1, CLUSTER), score_scale)
    moved_f = shifted(attended.reshape(1, block_rows, group_features), "pipe", 1)
    rows_b = gather_block(arrived_b, next_b[1])
    shared_grad, value_grad = backward_block(
        rows_b[0], rows_b[1], rows_b[2], next_b[2].reshape(-1, CLUSTER), score_scale
    )
    results_b = jnp.stack([shared_grad, value_grad]).reshape(2, block_rows, group_features)
    results_b = jnp.where(last_plane, jnp.zeros_like(results_b), results_b)
    shared_grad_in, values_grad_in, forward_in = give_back(
        jnp.concatenate([results_b, moved_f]),
        jnp.stack([next_b[1]] * 2 + [prev_f[1]]),
        jnp.stack([next_b[0]] * 2 + [prev_f[0]]),
    )
    return (forward_in, shared_grad_in, values_grad_in)


def solution(mesh):
    in_specs = (
        P("pipe", ("seq", "mp"), None),
        P("pipe", ("seq", "mp"), None),
        P("pipe", ("seq", "mp"), None),
        P("pipe", ("seq", "mp"), None),
        P("pipe", ("seq", "mp"), None),
        P("pipe", None, None),
    )
    out_specs = (
        P("pipe", ("seq", "mp"), None),
        P("pipe", ("seq", "mp"), None),
        P("pipe", ("seq", "mp"), None),
    )
    return jax.shard_map(
        per_device, mesh=mesh, in_specs=in_specs, out_specs=out_specs, check_vma=False
    )
```

```python
import math

import jax
import jax.numpy as jnp
from jax import lax
from jax.sharding import PartitionSpec as P

HEAD_DIM = 128
CLUSTER = 256


MASKED = -1e30


def shifted(block, axis, distance):
    devices = range(lax.axis_size(axis))
    route = [(i - distance, i) for i in devices if i - distance in devices]
    return lax.ppermute(block, axis, route)


def visible_mask(positions):
    count = positions.shape[1]
    earlier = positions[:, None, :] < positions[:, :, None]
    earliest = positions == jnp.min(positions, axis=1, keepdims=True)
    diagonal = (jnp.arange(count)[:, None] == jnp.arange(count)[None, :])[None]
    return earlier | diagonal & earliest[:, :, None]


def softmax_weights(shared, positions, score_scale):
    scores = (
        jnp.einsum("nqhd,nkhd->nhqk", shared, shared, preferred_element_type=jnp.float32)
        * score_scale
    )
    scores = jnp.where(visible_mask(positions)[:, None], scores, MASKED)
    largest = jnp.max(scores, axis=-1, keepdims=True)
    exponent = jnp.exp(scores - largest)
    return exponent / jnp.sum(exponent, axis=-1, keepdims=True)


def forward_block(shared, values, positions, score_scale):
    weights = softmax_weights(shared, positions, score_scale).astype(jnp.bfloat16)
    return jnp.einsum(
        "nhqk,nkhd->nqhd", weights, values, preferred_element_type=jnp.float32
    ).astype(jnp.bfloat16)


def backward_block(shared, values, upstream, positions, score_scale):
    weights = softmax_weights(shared, positions, score_scale)
    rounded = weights.astype(jnp.bfloat16)
    output_b = jnp.einsum("nhqk,nkhd->nqhd", rounded, values, preferred_element_type=jnp.float32)
    row_delta = jnp.sum(upstream.astype(jnp.float32) * output_b, axis=-1)
    value_grad = jnp.einsum(
        "nhqk,nqhd->nkhd", rounded, upstream, preferred_element_type=jnp.float32
    ).astype(jnp.bfloat16)
    prob_grad = jnp.einsum("nqhd,nkhd->nhqk", upstream, values, preferred_element_type=jnp.float32)
    score_grad = (
        weights * (prob_grad - jnp.transpose(row_delta, (0, 2, 1))[..., None]) * score_scale
    ).astype(jnp.bfloat16)
    shared_grad = jnp.einsum(
        "nhqk,nkhd->nqhd", score_grad, shared, preferred_element_type=jnp.float32
    )
    shared_grad = shared_grad + jnp.einsum(
        "nhqk,nqhd->nkhd", score_grad, shared, preferred_element_type=jnp.float32
    )
    return (shared_grad.astype(jnp.bfloat16), value_grad)


def route_plan(slot_tokens, seq_index, range_here, seq_count, group_count, tok_dev, slot_count):
    block_rows = slot_tokens.shape[0] // seq_count
    source = slot_tokens // tok_dev
    local_row = (slot_tokens - range_here * tok_dev).reshape(seq_count, block_rows)
    owned_here = (source == range_here).reshape(seq_count, block_rows)
    slot_rank = jnp.cumsum(owned_here.astype(jnp.int32), axis=1) - 1
    selected = owned_here[:, None, :] & (
        slot_rank[:, None, :] == jnp.arange(slot_count)[None, :, None]
    )
    send_rows = jnp.sum(jnp.where(selected, local_row[:, None, :], 0), axis=2)
    filled = jnp.any(selected, axis=2)
    send = filled[:, :, None] & (send_rows[:, :, None] == jnp.arange(tok_dev)[None, None, :])
    block_order = lax.dynamic_slice_in_dim(slot_tokens, seq_index * block_rows, block_rows)
    block_source = block_order // tok_dev
    indicator = (block_source[:, None] == jnp.arange(group_count)[None, :]).astype(jnp.int32)
    block_rank = jnp.sum(jnp.cumsum(indicator, axis=0) * indicator, axis=1) - 1
    gather = (block_source[:, None, None] == jnp.arange(group_count)[None, :, None]) & (
        block_rank[:, None, None] == jnp.arange(slot_count)[None, None, :]
    )
    return (
        send.astype(jnp.bfloat16),
        gather.astype(jnp.bfloat16),
        block_order,
    )


def per_device(shared_fwd, values_fwd, shared_bwd, values_bwd, upstream_bwd, cluster_order):
    seq_count = lax.axis_size("seq")
    mp_count = lax.axis_size("mp")
    seq_index = lax.axis_index("seq")
    mp_index = lax.axis_index("mp")
    tok_dev = shared_fwd.shape[1]
    features = shared_fwd.shape[2]
    group_features = features // mp_count
    heads_dev = group_features // HEAD_DIM
    group_count = seq_count * mp_count
    range_here = seq_index * mp_count + mp_index
    block_rows = cluster_order.shape[2] // seq_count
    slot_count = 2 * block_rows // group_count
    score_scale = 1.0 / math.sqrt(HEAD_DIM)
    axes = ("seq", "mp")
    pipe_index = lax.axis_index("pipe")
    last_plane = pipe_index == lax.axis_size("pipe") - 1
    order_fwd = cluster_order[0, 0]
    order_next_bwd = shifted(cluster_order[0, 1], "pipe", -1)
    inputs_b = shifted(jnp.concatenate([shared_bwd, values_bwd, upstream_bwd]), "pipe", -1)
    shared_bwd, values_bwd, upstream_bwd = inputs_b[0:1], inputs_b[1:2], inputs_b[2:3]
    order_prev_fwd = shifted(order_fwd, "pipe", 1)

    def plan(order):
        return route_plan(order, seq_index, range_here, seq_count, group_count, tok_dev, slot_count)

    own_f, next_b, prev_f = plan(order_fwd), plan(order_next_bwd), plan(order_prev_fwd)

    def exchange(arrays, send):
        packed = [
            jnp.einsum("skt,tf->skf", send, array[0], preferred_element_type=jnp.bfloat16)
            for array in arrays
        ]
        stacked = jnp.stack(packed, axis=1).reshape(
            seq_count, len(arrays), slot_count, mp_count, group_features
        )
        stacked = jnp.transpose(stacked, (0, 3, 1, 2, 4)).reshape(
            group_count, len(arrays), slot_count, group_features
        )
        arrived = lax.all_to_all(stacked, axes, split_axis=0, concat_axis=0, tiled=True)
        return arrived

    def gather_block(arrived, gather):
        rows = jnp.einsum("irk,rakf->aif", gather, arrived, preferred_element_type=jnp.bfloat16)
        return rows.reshape(rows.shape[0], 1, block_rows, heads_dev, HEAD_DIM)

    def give_back(results, gather, send):
        placed = jnp.einsum("airk,aif->rakf", gather, results, preferred_element_type=jnp.bfloat16)
        arrived = lax.all_to_all(placed, axes, split_axis=0, concat_axis=0, tiled=True)
        arrived = arrived.reshape(seq_count, mp_count, results.shape[0], slot_count, group_features)
        rows = jnp.einsum("askt,smakf->atmf", send, arrived, preferred_element_type=jnp.bfloat16)
        return [row.reshape(1, tok_dev, features) for row in rows]

    arrived_f = exchange((shared_fwd, values_fwd), own_f[0])
    rows_f = gather_block(arrived_f, own_f[1])
    arrived_b = exchange((shared_bwd, values_bwd, upstream_bwd), next_b[0])
    attended = forward_block(rows_f[0], rows_f[1], own_f[2].reshape(-1, CLUSTER), score_scale)
    moved_f = shifted(attended.reshape(1, block_rows, group_features), "pipe", 1)
    (forward_in,) = give_back(moved_f, prev_f[1][None], prev_f[0][None])
    rows_b = gather_block(arrived_b, next_b[1])
    shared_grad, value_grad = backward_block(
        rows_b[0], rows_b[1], rows_b[2], next_b[2].reshape(-1, CLUSTER), score_scale
    )
    results_b = jnp.stack([shared_grad, value_grad]).reshape(2, block_rows, group_features)
    results_b = jnp.where(last_plane, jnp.zeros_like(results_b), results_b)
    shared_grad_in, values_grad_in = give_back(
        results_b, jnp.stack([next_b[1]] * 2), jnp.stack([next_b[0]] * 2)
    )
    return (forward_in, shared_grad_in, values_grad_in)


def solution(mesh):
    in_specs = (
        P("pipe", ("seq", "mp"), None),
        P("pipe", ("seq", "mp"), None),
        P("pipe", ("seq", "mp"), None),
        P("pipe", ("seq", "mp"), None),
        P("pipe", ("seq", "mp"), None),
        P("pipe", None, None),
    )
    out_specs = (
        P("pipe", ("seq", "mp"), None),
        P("pipe", ("seq", "mp"), None),
        P("pipe", ("seq", "mp"), None),
    )
    return jax.shard_map(
        per_device, mesh=mesh, in_specs=in_specs, out_specs=out_specs, check_vma=False
    )
```

```python
import math

import jax
import jax.numpy as jnp
from jax import lax
from jax.sharding import PartitionSpec as P

HEAD_DIM = 128
CLUSTER = 256


MASKED = -1e30


def shifted(block, axis, distance):
    devices = range(lax.axis_size(axis))
    route = [(i - distance, i) for i in devices if i - distance in devices]
    return lax.ppermute(block, axis, route)


def visible_mask(positions):
    count = positions.shape[1]
    earlier = positions[:, None, :] < positions[:, :, None]
    earliest = positions == jnp.min(positions, axis=1, keepdims=True)
    diagonal = (jnp.arange(count)[:, None] == jnp.arange(count)[None, :])[None]
    return earlier | diagonal & earliest[:, :, None]


def softmax_weights(shared, positions, score_scale):
    scores = (
        jnp.einsum("nqhd,nkhd->nhqk", shared, shared, preferred_element_type=jnp.float32)
        * score_scale
    )
    scores = jnp.where(visible_mask(positions)[:, None], scores, MASKED)
    largest = jnp.max(scores, axis=-1, keepdims=True)
    exponent = jnp.exp(scores - largest)
    return exponent / jnp.sum(exponent, axis=-1, keepdims=True)


def forward_block(shared, values, positions, score_scale):
    weights = softmax_weights(shared, positions, score_scale).astype(jnp.bfloat16)
    return jnp.einsum(
        "nhqk,nkhd->nqhd", weights, values, preferred_element_type=jnp.float32
    ).astype(jnp.bfloat16)


def backward_block(shared, values, upstream, positions, score_scale):
    weights = softmax_weights(shared, positions, score_scale)
    rounded = weights.astype(jnp.bfloat16)
    output_b = jnp.einsum("nhqk,nkhd->nqhd", rounded, values, preferred_element_type=jnp.float32)
    row_delta = jnp.sum(upstream.astype(jnp.float32) * output_b, axis=-1)
    value_grad = jnp.einsum(
        "nhqk,nqhd->nkhd", rounded, upstream, preferred_element_type=jnp.float32
    ).astype(jnp.bfloat16)
    prob_grad = jnp.einsum("nqhd,nkhd->nhqk", upstream, values, preferred_element_type=jnp.float32)
    score_grad = (
        weights * (prob_grad - jnp.transpose(row_delta, (0, 2, 1))[..., None]) * score_scale
    ).astype(jnp.bfloat16)
    shared_grad = jnp.einsum(
        "nhqk,nkhd->nqhd", score_grad, shared, preferred_element_type=jnp.float32
    )
    shared_grad = shared_grad + jnp.einsum(
        "nhqk,nqhd->nkhd", score_grad, shared, preferred_element_type=jnp.float32
    )
    return (shared_grad.astype(jnp.bfloat16), value_grad)


def route_plan(slot_tokens, seq_index, range_here, seq_count, group_count, tok_dev, slot_count):
    block_rows = slot_tokens.shape[0] // seq_count
    source = slot_tokens // tok_dev
    local_row = (slot_tokens - range_here * tok_dev).reshape(seq_count, block_rows)
    owned_here = (source == range_here).reshape(seq_count, block_rows)
    slot_rank = jnp.cumsum(owned_here.astype(jnp.int32), axis=1) - 1
    selected = owned_here[:, None, :] & (
        slot_rank[:, None, :] == jnp.arange(slot_count)[None, :, None]
    )
    send_rows = jnp.sum(jnp.where(selected, local_row[:, None, :], 0), axis=2)
    filled = jnp.any(selected, axis=2)
    send = filled[:, :, None] & (send_rows[:, :, None] == jnp.arange(tok_dev)[None, None, :])
    block_order = lax.dynamic_slice_in_dim(slot_tokens, seq_index * block_rows, block_rows)
    block_source = block_order // tok_dev
    indicator = (block_source[:, None] == jnp.arange(group_count)[None, :]).astype(jnp.int32)
    block_rank = jnp.sum(jnp.cumsum(indicator, axis=0) * indicator, axis=1) - 1
    gather = (block_source[:, None, None] == jnp.arange(group_count)[None, :, None]) & (
        block_rank[:, None, None] == jnp.arange(slot_count)[None, None, :]
    )
    return (
        send.astype(jnp.bfloat16),
        gather.astype(jnp.bfloat16),
        block_order,
    )


def per_device(shared_fwd, values_fwd, shared_bwd, values_bwd, upstream_bwd, cluster_order):
    seq_count = lax.axis_size("seq")
    mp_count = lax.axis_size("mp")
    seq_index = lax.axis_index("seq")
    mp_index = lax.axis_index("mp")
    tok_dev = shared_fwd.shape[1]
    features = shared_fwd.shape[2]
    group_features = features // mp_count
    heads_dev = group_features // HEAD_DIM
    group_count = seq_count * mp_count
    range_here = seq_index * mp_count + mp_index
    block_rows = cluster_order.shape[2] // seq_count
    slot_count = 2 * block_rows // group_count
    score_scale = 1.0 / math.sqrt(HEAD_DIM)
    axes = ("seq", "mp")
    pipe_index = lax.axis_index("pipe")
    last_plane = pipe_index == lax.axis_size("pipe") - 1
    order_fwd = cluster_order[0, 0]
    order_next_bwd = shifted(cluster_order[0, 1], "pipe", -1)
    inputs_b = shifted(jnp.concatenate([shared_bwd, values_bwd, upstream_bwd]), "pipe", -1)
    shared_bwd, values_bwd, upstream_bwd = inputs_b[0:1], inputs_b[1:2], inputs_b[2:3]

    def plan(order):
        return route_plan(order, seq_index, range_here, seq_count, group_count, tok_dev, slot_count)

    own_f, next_b = plan(order_fwd), plan(order_next_bwd)

    def exchange(arrays, send):
        packed = [
            jnp.einsum("skt,tf->skf", send, array[0], preferred_element_type=jnp.bfloat16)
            for array in arrays
        ]
        stacked = jnp.stack(packed, axis=1).reshape(
            seq_count, len(arrays), slot_count, mp_count, group_features
        )
        stacked = jnp.transpose(stacked, (0, 3, 1, 2, 4)).reshape(
            group_count, len(arrays), slot_count, group_features
        )
        arrived = lax.all_to_all(stacked, axes, split_axis=0, concat_axis=0, tiled=True)
        return arrived

    def gather_block(arrived, gather):
        rows = jnp.einsum("irk,rakf->aif", gather, arrived, preferred_element_type=jnp.bfloat16)
        return rows.reshape(rows.shape[0], 1, block_rows, heads_dev, HEAD_DIM)

    def give_back(results, gather, send):
        placed = jnp.einsum("airk,aif->rakf", gather, results, preferred_element_type=jnp.bfloat16)
        arrived = lax.all_to_all(placed, axes, split_axis=0, concat_axis=0, tiled=True)
        arrived = arrived.reshape(seq_count, mp_count, results.shape[0], slot_count, group_features)
        rows = jnp.einsum("askt,smakf->atmf", send, arrived, preferred_element_type=jnp.bfloat16)
        return [row.reshape(1, tok_dev, features) for row in rows]

    arrived_f = exchange((shared_fwd, values_fwd), own_f[0])
    rows_f = gather_block(arrived_f, own_f[1])
    arrived_b = exchange((shared_bwd, values_bwd, upstream_bwd), next_b[0])
    attended = forward_block(rows_f[0], rows_f[1], own_f[2].reshape(-1, CLUSTER), score_scale)
    placed_f = jnp.einsum(
        "irk,if->rkf", own_f[1], attended.reshape(block_rows, group_features),
        preferred_element_type=jnp.bfloat16,
    ).reshape(group_count * slot_count, group_features)
    unpack = own_f[0].reshape(-1)
    extra = -(-unpack.shape[0] // group_features)
    unpack = jnp.pad(unpack, (0, extra * group_features - unpack.shape[0]))
    moved_f = shifted(
        jnp.concatenate([placed_f, unpack.reshape(extra, group_features)]), "pipe", 1
    )
    unpack_f = moved_f[group_count * slot_count :].reshape(-1)[: own_f[0].size].reshape(
        own_f[0].shape
    )
    placed_f = moved_f[: group_count * slot_count].reshape(
        group_count, 1, slot_count, group_features
    )
    arrived_f = lax.all_to_all(placed_f, axes, split_axis=0, concat_axis=0, tiled=True)
    arrived_f = arrived_f.reshape(seq_count, mp_count, 1, slot_count, group_features)
    forward_in = jnp.einsum(
        "skt,smakf->atmf", unpack_f, arrived_f, preferred_element_type=jnp.bfloat16
    ).reshape(1, tok_dev, features)
    rows_b = gather_block(arrived_b, next_b[1])
    shared_grad, value_grad = backward_block(
        rows_b[0], rows_b[1], rows_b[2], next_b[2].reshape(-1, CLUSTER), score_scale
    )
    results_b = jnp.stack([shared_grad, value_grad]).reshape(2, block_rows, group_features)
    results_b = jnp.where(last_plane, jnp.zeros_like(results_b), results_b)
    shared_grad_in, values_grad_in = give_back(
        results_b, jnp.stack([next_b[1]] * 2), jnp.stack([next_b[0]] * 2)
    )
    return (forward_in, shared_grad_in, values_grad_in)


def solution(mesh):
    in_specs = (
        P("pipe", ("seq", "mp"), None),
        P("pipe", ("seq", "mp"), None),
        P("pipe", ("seq", "mp"), None),
        P("pipe", ("seq", "mp"), None),
        P("pipe", ("seq", "mp"), None),
        P("pipe", None, None),
    )
    out_specs = (
        P("pipe", ("seq", "mp"), None),
        P("pipe", ("seq", "mp"), None),
        P("pipe", ("seq", "mp"), None),
    )
    return jax.shard_map(
        per_device, mesh=mesh, in_specs=in_specs, out_specs=out_specs, check_vma=False
    )
```

```python
import math

import jax
import jax.numpy as jnp
from jax import lax
from jax.sharding import PartitionSpec as P

HEAD_DIM = 128
CLUSTER = 256


MASKED = -1e30


def shifted(block, axis, distance):
    devices = range(lax.axis_size(axis))
    route = [(i - distance, i) for i in devices if i - distance in devices]
    return lax.ppermute(block, axis, route)


def visible_mask(positions):
    count = positions.shape[1]
    earlier = positions[:, None, :] < positions[:, :, None]
    earliest = positions == jnp.min(positions, axis=1, keepdims=True)
    diagonal = (jnp.arange(count)[:, None] == jnp.arange(count)[None, :])[None]
    return earlier | diagonal & earliest[:, :, None]


def softmax_weights(shared, positions, score_scale):
    scores = (
        jnp.einsum("nqhd,nkhd->nhqk", shared, shared, preferred_element_type=jnp.float32)
        * score_scale
    )
    scores = jnp.where(visible_mask(positions)[:, None], scores, MASKED)
    largest = jnp.max(scores, axis=-1, keepdims=True)
    exponent = jnp.exp(scores - largest)
    return exponent / jnp.sum(exponent, axis=-1, keepdims=True)


def forward_block(shared, values, positions, score_scale):
    weights = softmax_weights(shared, positions, score_scale).astype(jnp.bfloat16)
    return jnp.einsum(
        "nhqk,nkhd->nqhd", weights, values, preferred_element_type=jnp.float32
    ).astype(jnp.bfloat16)


def backward_block(shared, values, upstream, positions, score_scale):
    weights = softmax_weights(shared, positions, score_scale)
    rounded = weights.astype(jnp.bfloat16)
    output_b = jnp.einsum("nhqk,nkhd->nqhd", rounded, values, preferred_element_type=jnp.float32)
    row_delta = jnp.sum(upstream.astype(jnp.float32) * output_b, axis=-1)
    value_grad = jnp.einsum(
        "nhqk,nqhd->nkhd", rounded, upstream, preferred_element_type=jnp.float32
    ).astype(jnp.bfloat16)
    prob_grad = jnp.einsum("nqhd,nkhd->nhqk", upstream, values, preferred_element_type=jnp.float32)
    score_grad = (
        weights * (prob_grad - jnp.transpose(row_delta, (0, 2, 1))[..., None]) * score_scale
    ).astype(jnp.bfloat16)
    shared_grad = jnp.einsum(
        "nhqk,nkhd->nqhd", score_grad, shared, preferred_element_type=jnp.float32
    )
    shared_grad = shared_grad + jnp.einsum(
        "nhqk,nqhd->nkhd", score_grad, shared, preferred_element_type=jnp.float32
    )
    return (shared_grad.astype(jnp.bfloat16), value_grad)


def route_plan(slot_tokens, seq_index, range_here, seq_count, group_count, tok_dev, slot_count):
    block_rows = slot_tokens.shape[0] // seq_count
    source = slot_tokens // tok_dev
    local_row = (slot_tokens - range_here * tok_dev).reshape(seq_count, block_rows)
    owned_here = (source == range_here).reshape(seq_count, block_rows)
    slot_rank = jnp.cumsum(owned_here.astype(jnp.int32), axis=1) - 1
    selected = owned_here[:, None, :] & (
        slot_rank[:, None, :] == jnp.arange(slot_count)[None, :, None]
    )
    send_rows = jnp.sum(jnp.where(selected, local_row[:, None, :], 0), axis=2)
    filled = jnp.any(selected, axis=2)
    send = filled[:, :, None] & (send_rows[:, :, None] == jnp.arange(tok_dev)[None, None, :])
    block_order = lax.dynamic_slice_in_dim(slot_tokens, seq_index * block_rows, block_rows)
    block_source = block_order // tok_dev
    indicator = (block_source[:, None] == jnp.arange(group_count)[None, :]).astype(jnp.int32)
    block_rank = jnp.sum(jnp.cumsum(indicator, axis=0) * indicator, axis=1) - 1
    gather = (block_source[:, None, None] == jnp.arange(group_count)[None, :, None]) & (
        block_rank[:, None, None] == jnp.arange(slot_count)[None, None, :]
    )
    return (
        send.astype(jnp.bfloat16),
        gather.astype(jnp.bfloat16),
        block_order,
    )


def per_device(shared_fwd, values_fwd, shared_bwd, values_bwd, upstream_bwd, cluster_order):
    seq_count = lax.axis_size("seq")
    mp_count = lax.axis_size("mp")
    seq_index = lax.axis_index("seq")
    mp_index = lax.axis_index("mp")
    tok_dev = shared_fwd.shape[1]
    features = shared_fwd.shape[2]
    group_features = features // mp_count
    heads_dev = group_features // HEAD_DIM
    group_count = seq_count * mp_count
    range_here = seq_index * mp_count + mp_index
    block_rows = cluster_order.shape[2] // seq_count
    slot_count = 2 * block_rows // group_count
    score_scale = 1.0 / math.sqrt(HEAD_DIM)
    axes = ("seq", "mp")
    pipe_index = lax.axis_index("pipe")
    last_plane = pipe_index == lax.axis_size("pipe") - 1
    order_fwd = cluster_order[0, 0]
    order_next_bwd = shifted(cluster_order[0, 1], "pipe", -1)
    inputs_b = shifted(jnp.concatenate([shared_bwd, values_bwd, upstream_bwd]), "pipe", -1)
    shared_bwd, values_bwd, upstream_bwd = inputs_b[0:1], inputs_b[1:2], inputs_b[2:3]

    def plan(order):
        return route_plan(order, seq_index, range_here, seq_count, group_count, tok_dev, slot_count)

    own_f, next_b = plan(order_fwd), plan(order_next_bwd)

    def exchange(arrays, send):
        packed = [
            jnp.einsum("skt,tf->skf", send, array[0], preferred_element_type=jnp.bfloat16)
            for array in arrays
        ]
        stacked = jnp.stack(packed, axis=1).reshape(
            seq_count, len(arrays), slot_count, mp_count, group_features
        )
        stacked = jnp.transpose(stacked, (0, 3, 1, 2, 4)).reshape(
            group_count, len(arrays), slot_count, group_features
        )
        arrived = lax.all_to_all(stacked, axes, split_axis=0, concat_axis=0, tiled=True)
        return arrived

    def gather_block(arrived, gather):
        rows = jnp.einsum("irk,rakf->aif", gather, arrived, preferred_element_type=jnp.bfloat16)
        return rows.reshape(rows.shape[0], 1, block_rows, heads_dev, HEAD_DIM)

    def give_back(results, gather, send):
        placed = jnp.einsum("airk,aif->rakf", gather, results, preferred_element_type=jnp.bfloat16)
        arrived = lax.all_to_all(placed, axes, split_axis=0, concat_axis=0, tiled=True)
        arrived = arrived.reshape(seq_count, mp_count, results.shape[0], slot_count, group_features)
        rows = jnp.einsum("askt,smakf->atmf", send, arrived, preferred_element_type=jnp.bfloat16)
        return [row.reshape(1, tok_dev, features) for row in rows]

    arrived_f = exchange((shared_fwd, values_fwd), own_f[0])
    rows_f = gather_block(arrived_f, own_f[1])
    packed_b = jnp.einsum(
        "skt,atf->skaf", next_b[0], inputs_b, preferred_element_type=jnp.bfloat16
    ).reshape(seq_count, slot_count, 3, mp_count, group_features)
    packed_b = jnp.transpose(packed_b, (0, 3, 2, 1, 4)).reshape(
        group_count, 3, slot_count, group_features
    )
    arrived_b = lax.all_to_all(packed_b, axes, split_axis=0, concat_axis=0, tiled=True)
    attended = forward_block(rows_f[0], rows_f[1], own_f[2].reshape(-1, CLUSTER), score_scale)
    placed_f = jnp.einsum(
        "irk,if->rkf", own_f[1], attended.reshape(block_rows, group_features),
        preferred_element_type=jnp.bfloat16,
    ).reshape(group_count * slot_count, group_features)
    unpack = own_f[0].reshape(-1)
    extra = -(-unpack.shape[0] // group_features)
    unpack = jnp.pad(unpack, (0, extra * group_features - unpack.shape[0]))
    moved_f = shifted(
        jnp.concatenate([placed_f, unpack.reshape(extra, group_features)]), "pipe", 1
    )
    unpack_f = moved_f[group_count * slot_count :].reshape(-1)[: own_f[0].size].reshape(
        own_f[0].shape
    )
    placed_f = moved_f[: group_count * slot_count].reshape(
        group_count, 1, slot_count, group_features
    )
    arrived_f = lax.all_to_all(placed_f, axes, split_axis=0, concat_axis=0, tiled=True)
    arrived_f = arrived_f.reshape(seq_count, mp_count, 1, slot_count, group_features)
    forward_in = jnp.einsum(
        "skt,smakf->atmf", unpack_f, arrived_f, preferred_element_type=jnp.bfloat16
    ).reshape(1, tok_dev, features)
    rows_b = gather_block(arrived_b, next_b[1])
    shared_grad, value_grad = backward_block(
        rows_b[0], rows_b[1], rows_b[2], next_b[2].reshape(-1, CLUSTER), score_scale
    )
    results_b = jnp.stack([shared_grad, value_grad]).reshape(2, block_rows, group_features)
    results_b = jnp.where(last_plane, jnp.zeros_like(results_b), results_b)
    shared_grad_in, values_grad_in = give_back(
        results_b, jnp.stack([next_b[1]] * 2), jnp.stack([next_b[0]] * 2)
    )
    return (forward_in, shared_grad_in, values_grad_in)


def solution(mesh):
    in_specs = (
        P("pipe", ("seq", "mp"), None),
        P("pipe", ("seq", "mp"), None),
        P("pipe", ("seq", "mp"), None),
        P("pipe", ("seq", "mp"), None),
        P("pipe", ("seq", "mp"), None),
        P("pipe", None, None),
    )
    out_specs = (
        P("pipe", ("seq", "mp"), None),
        P("pipe", ("seq", "mp"), None),
        P("pipe", ("seq", "mp"), None),
    )
    return jax.shard_map(
        per_device, mesh=mesh, in_specs=in_specs, out_specs=out_specs, check_vma=False
    )
```

```python
import math

import jax
import jax.numpy as jnp
from jax import lax
from jax.sharding import PartitionSpec as P

HEAD_DIM = 128
CLUSTER = 256


MASKED = -1e30


def shifted(block, axis, distance):
    devices = range(lax.axis_size(axis))
    route = [(i - distance, i) for i in devices if i - distance in devices]
    return lax.ppermute(block, axis, route)


def visible_mask(positions):
    count = positions.shape[1]
    earlier = positions[:, None, :] < positions[:, :, None]
    earliest = positions == jnp.min(positions, axis=1, keepdims=True)
    diagonal = (jnp.arange(count)[:, None] == jnp.arange(count)[None, :])[None]
    return earlier | diagonal & earliest[:, :, None]


def softmax_weights(shared, positions, score_scale):
    scores = (
        jnp.einsum("nqhd,nkhd->nhqk", shared, shared, preferred_element_type=jnp.float32)
        * score_scale
    )
    scores = jnp.where(visible_mask(positions)[:, None], scores, MASKED)
    largest = jnp.max(scores, axis=-1, keepdims=True)
    exponent = jnp.exp(scores - largest)
    return exponent / jnp.sum(exponent, axis=-1, keepdims=True)


def forward_block(shared, values, positions, score_scale):
    weights = softmax_weights(shared, positions, score_scale).astype(jnp.bfloat16)
    return jnp.einsum(
        "nhqk,nkhd->nqhd", weights, values, preferred_element_type=jnp.float32
    ).astype(jnp.bfloat16)


def backward_block(shared, values, upstream, positions, score_scale):
    weights = softmax_weights(shared, positions, score_scale)
    rounded = weights.astype(jnp.bfloat16)
    output_b = jnp.einsum("nhqk,nkhd->nqhd", rounded, values, preferred_element_type=jnp.float32)
    row_delta = jnp.sum(upstream.astype(jnp.float32) * output_b, axis=-1)
    value_grad = jnp.einsum(
        "nhqk,nqhd->nkhd", rounded, upstream, preferred_element_type=jnp.float32
    ).astype(jnp.bfloat16)
    prob_grad = jnp.einsum("nqhd,nkhd->nhqk", upstream, values, preferred_element_type=jnp.float32)
    score_grad = (
        weights * (prob_grad - jnp.transpose(row_delta, (0, 2, 1))[..., None]) * score_scale
    ).astype(jnp.bfloat16)
    shared_grad = jnp.einsum(
        "nhqk,nkhd->nqhd", score_grad, shared, preferred_element_type=jnp.float32
    )
    shared_grad = shared_grad + jnp.einsum(
        "nhqk,nqhd->nkhd", score_grad, shared, preferred_element_type=jnp.float32
    )
    return (shared_grad.astype(jnp.bfloat16), value_grad)


def route_plan(slot_tokens, seq_index, range_here, seq_count, group_count, tok_dev, slot_count):
    block_rows = slot_tokens.shape[0] // seq_count
    source = slot_tokens // tok_dev
    local_row = (slot_tokens - range_here * tok_dev).reshape(seq_count, block_rows)
    owned_here = (source == range_here).reshape(seq_count, block_rows)
    slot_rank = jnp.cumsum(owned_here.astype(jnp.int32), axis=1) - 1
    selected = owned_here[:, None, :] & (
        slot_rank[:, None, :] == jnp.arange(slot_count)[None, :, None]
    )
    send_rows = jnp.sum(jnp.where(selected, local_row[:, None, :], 0), axis=2)
    filled = jnp.any(selected, axis=2)
    send = filled[:, :, None] & (send_rows[:, :, None] == jnp.arange(tok_dev)[None, None, :])
    block_order = lax.dynamic_slice_in_dim(slot_tokens, seq_index * block_rows, block_rows)
    block_source = block_order // tok_dev
    indicator = (block_source[:, None] == jnp.arange(group_count)[None, :]).astype(jnp.int32)
    block_rank = jnp.sum(jnp.cumsum(indicator, axis=0) * indicator, axis=1) - 1
    gather = (block_source[:, None, None] == jnp.arange(group_count)[None, :, None]) & (
        block_rank[:, None, None] == jnp.arange(slot_count)[None, None, :]
    )
    return (
        send.astype(jnp.bfloat16),
        gather.astype(jnp.bfloat16),
        block_order,
    )


def per_device(shared_fwd, values_fwd, shared_bwd, values_bwd, upstream_bwd, cluster_order):
    seq_count = lax.axis_size("seq")
    mp_count = lax.axis_size("mp")
    seq_index = lax.axis_index("seq")
    mp_index = lax.axis_index("mp")
    tok_dev = shared_fwd.shape[1]
    features = shared_fwd.shape[2]
    group_features = features // mp_count
    heads_dev = group_features // HEAD_DIM
    group_count = seq_count * mp_count
    range_here = seq_index * mp_count + mp_index
    block_rows = cluster_order.shape[2] // seq_count
    slot_count = 2 * block_rows // group_count
    score_scale = 1.0 / math.sqrt(HEAD_DIM)
    axes = ("seq", "mp")
    pipe_index = lax.axis_index("pipe")
    last_plane = pipe_index == lax.axis_size("pipe") - 1
    order_fwd = cluster_order[0, 0]
    order_next_bwd = shifted(cluster_order[0, 1], "pipe", -1)
    shared_bwd, values_bwd, upstream_bwd = shifted((shared_bwd, values_bwd, upstream_bwd), "pipe", -1)

    def plan(order):
        return route_plan(order, seq_index, range_here, seq_count, group_count, tok_dev, slot_count)

    own_f, next_b = plan(order_fwd), plan(order_next_bwd)

    def exchange(arrays, send):
        packed = [
            jnp.einsum("skt,tf->skf", send, array[0], preferred_element_type=jnp.bfloat16)
            for array in arrays
        ]
        stacked = jnp.stack(packed, axis=1).reshape(
            seq_count, len(arrays), slot_count, mp_count, group_features
        )
        stacked = jnp.transpose(stacked, (0, 3, 1, 2, 4)).reshape(
            group_count, len(arrays), slot_count, group_features
        )
        arrived = lax.all_to_all(stacked, axes, split_axis=0, concat_axis=0, tiled=True)
        return arrived

    def gather_block(arrived, gather):
        rows = jnp.einsum("irk,rakf->aif", gather, arrived, preferred_element_type=jnp.bfloat16)
        return rows.reshape(rows.shape[0], 1, block_rows, heads_dev, HEAD_DIM)

    def give_back(results, gather, send):
        placed = jnp.einsum("airk,aif->rakf", gather, results, preferred_element_type=jnp.bfloat16)
        arrived = lax.all_to_all(placed, axes, split_axis=0, concat_axis=0, tiled=True)
        arrived = arrived.reshape(seq_count, mp_count, results.shape[0], slot_count, group_features)
        rows = jnp.einsum("askt,smakf->atmf", send, arrived, preferred_element_type=jnp.bfloat16)
        return [row.reshape(1, tok_dev, features) for row in rows]

    arrived_f = exchange((shared_fwd, values_fwd), own_f[0])
    rows_f = gather_block(arrived_f, own_f[1])
    arrived_b = exchange((shared_bwd, values_bwd, upstream_bwd), next_b[0])
    attended = forward_block(rows_f[0], rows_f[1], own_f[2].reshape(-1, CLUSTER), score_scale)
    placed_f = jnp.einsum(
        "irk,if->rkf", own_f[1], attended.reshape(block_rows, group_features),
        preferred_element_type=jnp.bfloat16,
    ).reshape(group_count * slot_count, group_features)
    unpack = own_f[0].reshape(-1)
    extra = -(-unpack.shape[0] // group_features)
    unpack = jnp.pad(unpack, (0, extra * group_features - unpack.shape[0]))
    moved_f = shifted(
        jnp.concatenate([placed_f, unpack.reshape(extra, group_features)]), "pipe", 1
    )
    unpack_f = moved_f[group_count * slot_count :].reshape(-1)[: own_f[0].size].reshape(
        own_f[0].shape
    )
    placed_f = moved_f[: group_count * slot_count].reshape(
        group_count, 1, slot_count, group_features
    )
    arrived_f = lax.all_to_all(placed_f, axes, split_axis=0, concat_axis=0, tiled=True)
    arrived_f = arrived_f.reshape(seq_count, mp_count, 1, slot_count, group_features)
    forward_in = jnp.einsum(
        "skt,smakf->atmf", unpack_f, arrived_f, preferred_element_type=jnp.bfloat16
    ).reshape(1, tok_dev, features)
    rows_b = gather_block(arrived_b, next_b[1])
    shared_grad, value_grad = backward_block(
        rows_b[0], rows_b[1], rows_b[2], next_b[2].reshape(-1, CLUSTER), score_scale
    )
    results_b = jnp.stack([shared_grad, value_grad]).reshape(2, block_rows, group_features)
    results_b = jnp.where(last_plane, jnp.zeros_like(results_b), results_b)
    shared_grad_in, values_grad_in = give_back(
        results_b, jnp.stack([next_b[1]] * 2), jnp.stack([next_b[0]] * 2)
    )
    return (forward_in, shared_grad_in, values_grad_in)


def solution(mesh):
    in_specs = (
        P("pipe", ("seq", "mp"), None),
        P("pipe", ("seq", "mp"), None),
        P("pipe", ("seq", "mp"), None),
        P("pipe", ("seq", "mp"), None),
        P("pipe", ("seq", "mp"), None),
        P("pipe", None, None),
    )
    out_specs = (
        P("pipe", ("seq", "mp"), None),
        P("pipe", ("seq", "mp"), None),
        P("pipe", ("seq", "mp"), None),
    )
    return jax.shard_map(
        per_device, mesh=mesh, in_specs=in_specs, out_specs=out_specs, check_vma=False
    )
```
